32 devices in a mesh: groups: 2 (over x), ctx: 8 (over z, y), head: 2 (over core).
Axes of the slice: x: 2, y: 2, z: 4, core: 2. Of those that a mesh axis runs over, the one named last changes fastest.
Arguments:
- queries: bfloat16 [2048, 8192], P(('groups', 'ctx'), 'head'), parts along dimension 0, may hold values from -6 to 6
- key_rows: bfloat16 [2048, 1024], P(('groups', 'ctx'), 'head'), parts along dimension 0, may hold values from -6 to 6
- value_rows: bfloat16 [2048, 1024], P(('groups', 'ctx'), 'head'), parts along dimension 0, may hold values from -6 to 6
- out_grad: bfloat16 [2048, 8192], P(('groups', 'ctx'), 'head'), parts along dimension 0, may hold values from -6 to 6
- doc_start: int32 [2048], P(('groups', 'ctx')), parts along dimension 0, may hold values from 0 to 1023, as said below
- span_order: int32 [32], P('groups'), parts along dimension 0, may hold values from 0 to 15, as said below
Outputs:
- attended: bfloat16 [2048, 8192], P(('groups', 'ctx'), 'head'), parts along dimension 0
- query_grad: bfloat16 [2048, 8192], P(('groups', 'ctx'), 'head'), parts along dimension 0
- key_grad: bfloat16 [2048, 1024], P(('groups', 'ctx'), 'head'), parts along dimension 0
- value_grad: bfloat16 [2048, 1024], P(('groups', 'ctx'), 'head'), parts along dimension 0
The draws below stay inside these ranges and needn't reach their ends.
There are 2 independent parts, one for each index of `groups`. The reference program is written for one: setup_inputs(seed, part) draws one part's arguments, and reference() takes and returns one part's arrays. A program takes and returns all parts, laid end to end along the dimension named above; each array names one. Nothing has to cross between parts.
Inputs may be any that keep to these rules, and one draw needn't show every extreme that they name: `span_order`: a permutation of the 16 spans. Documents are contiguous runs of sequence positions of at most 256, and one document is exactly 256 long; the last position is a document of its own; every row's doc_start is at most its own position.
All inputs are finite; a program needn't handle non-finite values.
Results may differ from the reference program's by a relative error of at most 0.0086.
Values may be sent and summed in bfloat16 or wider, within the bound.
No kernel may reach another device: no remote copies, remote signals or barrier semaphores. Data moves between devices by JAX's collectives and lax.ppermute only.
A program may use at most 64 MiB of HBM per device.

```python
import math
import jax
import jax.numpy as jnp
from jax import lax

H = 64
KV = 8
DH = 128
SPAN = 64
SEQ = 1024
NCHUNK = 16
MOST_DOC = 256
GROUP = 8


def layout(key):
    span_slots = jax.random.permutation(jax.random.fold_in(key, 11), NCHUNK).astype(jnp.int32)
    doc_lengths = jax.random.randint(jax.random.fold_in(key, 12), (SEQ,), 1, MOST_DOC + 1, dtype=jnp.int32)
    long_index = jax.random.randint(jax.random.fold_in(key, 13), (), 0, 2, dtype=jnp.int32)
    doc_lengths = jnp.where(jnp.arange(SEQ, dtype=jnp.int32) == long_index, MOST_DOC, doc_lengths).astype(jnp.int32)
    doc_ends = jnp.cumsum(doc_lengths).astype(jnp.int32)
    begins = (doc_ends - doc_lengths).astype(jnp.int32)
    places = jnp.arange(SEQ, dtype=jnp.int32)
    doc_index = jnp.searchsorted(doc_ends, places, side='right').astype(jnp.int32)
    starts_orig = jnp.where(places == SEQ - 1, SEQ - 1, begins[doc_index]).astype(jnp.int32)
    row_ids = jnp.arange(SEQ, dtype=jnp.int32)
    stored_pos = span_slots[row_ids // SPAN] * SPAN + row_ids % SPAN
    return (span_slots, starts_orig[stored_pos].astype(jnp.int32))


def draw_span_order(key, part):
    return layout(key)[0]


def draw_doc_start(key, part):
    return layout(key)[1]


def draw_queries(key, part):
    base_key = jax.random.fold_in(key, 21)
    drawn = jnp.clip(jax.random.normal(base_key, (SEQ, H * DH), jnp.float32), -6.0, 6.0)
    return drawn.astype(jnp.bfloat16)


def draw_key_rows(key, part):
    base_key = jax.random.fold_in(key, 22)
    drawn = jnp.clip(jax.random.normal(base_key, (SEQ, KV * DH), jnp.float32), -6.0, 6.0)
    return drawn.astype(jnp.bfloat16)


def shard_levels(key, shape, shards, least, largest):
    def one(position, parts):
        draws = jax.random.uniform(jax.random.fold_in(jax.random.fold_in(key, 6), position), (parts,), jnp.float32, least / len(shards), largest / len(shards))
        return jnp.repeat(jnp.exp(draws), shape[position] // parts).reshape((-1,) + (1,) * (len(shape) - position - 1))

    level = one(*shards[0])
    for cut in shards[1:]:
        level = level * one(*cut)
    return level


def centred(own_key, shape, scale, reach, shards=(), kind=jnp.bfloat16):
    array = scale * jax.random.normal(own_key, shape, jnp.float32)
    if shards:
        array = array * shard_levels(own_key, shape, shards, -0.22, 0.18)
    return jnp.clip(array, -reach, reach).astype(kind)


def setup_inputs(seed: int = 0, part: int = 0) -> dict:
    keys = jax.random.split(jax.random.key(seed), 7)
    own_keys = jax.random.split(jax.random.fold_in(keys[6], part), 7)
    return {
        "queries": draw_queries(jax.random.fold_in(jax.random.fold_in(keys[6], part), 71), part),
        "key_rows": draw_key_rows(jax.random.fold_in(jax.random.fold_in(keys[6], part), 71), part),
        "value_rows": centred(own_keys[2], (SEQ, KV * DH), 1.0, 6.0, ((0, 8), (1, 2))),
        "out_grad": centred(own_keys[3], (SEQ, H * DH), 1.0, 6.0, ((0, 8), (1, 2))),
        "doc_start": draw_doc_start(jax.random.fold_in(jax.random.fold_in(keys[6], part), 71), part),
        "span_order": draw_span_order(jax.random.fold_in(jax.random.fold_in(keys[6], part), 71), part),
    }


def stored_places(span_order):
    row_ids = jnp.arange(SEQ, dtype=jnp.int32)
    return (span_order[row_ids // SPAN] * SPAN + row_ids % SPAN).astype(jnp.int32)

def reference(queries, key_rows, value_rows, out_grad, doc_start, span_order):
    places = stored_places(span_order)
    visible_mask = (places[None, :] >= doc_start[:, None]) & (places[None, :] <= places[:, None])
    score_scale = 1.0 / math.sqrt(DH)
    query_heads = queries.reshape(SEQ, H, DH).transpose(1, 0, 2)
    key_heads = key_rows.reshape(SEQ, KV, DH).transpose(1, 0, 2)
    value_heads = value_rows.reshape(SEQ, KV, DH).transpose(1, 0, 2)
    grad_heads = out_grad.reshape(SEQ, H, DH).transpose(1, 0, 2)

    def one_head(head_index):
        query_block = query_heads[head_index]
        key_block = key_heads[head_index // GROUP]
        value_block = value_heads[head_index // GROUP]
        grad_block = grad_heads[head_index]
        scores = jnp.dot(query_block, key_block.T, preferred_element_type=jnp.float32) * score_scale
        masked = jnp.where(visible_mask, scores, -jnp.inf)
        row_max = lax.optimization_barrier(jnp.max(masked, axis=1))
        shifted = jnp.where(visible_mask, jnp.exp(masked - row_max[:, None]), 0.0)
        log_totals = row_max + jnp.log(lax.optimization_barrier(jnp.sum(shifted, axis=1)))
        weights = jnp.where(visible_mask, jnp.exp(masked - log_totals[:, None]), 0.0)
        weights_low = weights.astype(jnp.bfloat16)
        attended = jnp.dot(weights_low, value_block, preferred_element_type=jnp.float32).astype(jnp.bfloat16)
        row_dots = lax.optimization_barrier(jnp.sum(attended.astype(jnp.float32) * grad_block.astype(jnp.float32), axis=1))
        grad_weights = jnp.dot(grad_block, value_block.T, preferred_element_type=jnp.float32)
        grad_scores = (weights * (grad_weights - row_dots[:, None])).astype(jnp.bfloat16)
        query_grad = (jnp.dot(grad_scores, key_block, preferred_element_type=jnp.float32) * score_scale).astype(jnp.bfloat16)
        key_part = jnp.dot(grad_scores.T, query_block, preferred_element_type=jnp.float32) * score_scale
        value_part = jnp.dot(weights_low.T, grad_block, preferred_element_type=jnp.float32)
        return (attended, query_grad, key_part, value_part)
    attended, query_grad, key_parts, value_parts = lax.map(one_head, jnp.arange(H, dtype=jnp.int32))
    attended = attended.transpose(1, 0, 2).reshape(SEQ, H * DH)
    query_grad = query_grad.transpose(1, 0, 2).reshape(SEQ, H * DH)
    key_grad = key_parts.reshape(KV, GROUP, SEQ, DH).sum(axis=1).astype(jnp.bfloat16)
    value_grad = value_parts.reshape(KV, GROUP, SEQ, DH).sum(axis=1).astype(jnp.bfloat16)
    key_grad = key_grad.transpose(1, 0, 2).reshape(SEQ, KV * DH)
    value_grad = value_grad.transpose(1, 0, 2).reshape(SEQ, KV * DH)
    return (attended, query_grad, key_grad, value_grad)
```

```python
import math

import jax
import jax.numpy as jnp
from jax import lax
from jax.experimental import pallas as pl
from jax.experimental.pallas import tpu as pltpu
from jax.sharding import PartitionSpec as P

DH = 128
SPAN = 64


def attention_kernel(qpos_ref, qstart_ref, kpos_ref, q_ref, do_ref, k_ref, v_ref,
                     out_ref, dq_ref, dk_ref, dv_ref, *, group_size, score_scale):
    qpos = qpos_ref[...]
    qstart = qstart_ref[...]
    kpos = kpos_ref[0]
    visible = (kpos >= qstart) & (kpos <= qpos)
    key_block = k_ref[0]
    value_block = v_ref[0]
    window = key_block.shape[0]
    key_sum = jnp.zeros((window, DH), jnp.float32)
    value_sum = jnp.zeros((window, DH), jnp.float32)
    contract_last = (((1,), (1,)), ((), ()))
    contract_first = (((0,), (0,)), ((), ()))
    for head in range(group_size):
        cols = slice(head * DH, (head + 1) * DH)
        query_head = q_ref[:, cols]
        grad_head = do_ref[:, cols]
        scores = lax.dot_general(query_head, key_block, contract_last,
                                 preferred_element_type=jnp.float32) * score_scale
        masked = jnp.where(visible, scores, -jnp.inf)
        row_max = jnp.max(masked, axis=1, keepdims=True)
        shifted = jnp.where(visible, jnp.exp(masked - row_max), 0.0)
        log_totals = row_max + jnp.log(jnp.sum(shifted, axis=1, keepdims=True))
        weights = jnp.where(visible, jnp.exp(masked - log_totals), 0.0)
        weights_low = weights.astype(jnp.bfloat16)
        attended = jnp.dot(weights_low, value_block,
                           preferred_element_type=jnp.float32).astype(jnp.bfloat16)
        out_ref[:, cols] = attended
        row_dots = jnp.sum(attended.astype(jnp.float32) * grad_head.astype(jnp.float32),
                           axis=1, keepdims=True)
        grad_weights = lax.dot_general(grad_head, value_block, contract_last,
                                       preferred_element_type=jnp.float32)
        grad_scores = (weights * (grad_weights - row_dots)).astype(jnp.bfloat16)
        query_grad = jnp.dot(grad_scores, key_block, preferred_element_type=jnp.float32)
        dq_ref[:, cols] = (query_grad * score_scale).astype(jnp.bfloat16)
        key_sum = key_sum + lax.dot_general(grad_scores, query_head, contract_first,
                                            preferred_element_type=jnp.float32)
        value_sum = value_sum + lax.dot_general(weights_low, grad_head, contract_first,
                                                preferred_element_type=jnp.float32)
    dk_ref[0] = key_sum * score_scale
    dv_ref[0] = value_sum


def local(queries, key_rows, value_rows, out_grad, doc_start, span_order):
    local_rows = queries.shape[0]
    tiles = local_rows // SPAN
    head_count = queries.shape[1] // DH
    kv_count = key_rows.shape[1] // DH
    kv_cols = kv_count * DH
    group_size = head_count // kv_count
    group_cols = group_size * DH
    score_scale = 1.0 / math.sqrt(DH)
    ctx_count = lax.axis_size("ctx")
    my_index = lax.axis_index("ctx")
    total_rows = local_rows * ctx_count
    slot_count = total_rows // SPAN
    reach = total_rows // 4 // SPAN
    window_spans = reach + 1
    window = window_spans * SPAN

    slot_of_span = jnp.zeros((slot_count,), jnp.int32).at[span_order].set(
        jnp.arange(slot_count, dtype=jnp.int32))
    my_spans = lax.dynamic_slice_in_dim(span_order, my_index * tiles, tiles)
    window_span = my_spans[:, None] - reach + jnp.arange(window_spans, dtype=jnp.int32)[None, :]
    window_slot = slot_of_span[jnp.clip(window_span, 0, slot_count - 1)]
    row_in_span = jnp.arange(SPAN, dtype=jnp.int32)
    key_pos = (window_span[:, :, None] * SPAN + row_in_span[None, None, :]).reshape(tiles, 1, window)
    query_pos = (my_spans[:, None] * SPAN + row_in_span[None, :]).reshape(local_rows, 1)
    query_start = doc_start.reshape(local_rows, 1)

    key_all = lax.all_gather(key_rows, "ctx", axis=0, tiled=True).reshape(slot_count, SPAN, kv_cols)
    value_all = lax.all_gather(value_rows, "ctx", axis=0, tiled=True).reshape(slot_count, SPAN, kv_cols)
    key_win = key_all[window_slot].reshape(tiles, window, kv_cols)
    value_win = value_all[window_slot].reshape(tiles, window, kv_cols)

    kernel = pl.pallas_call(
        lambda *refs: attention_kernel(*refs, group_size=group_size, score_scale=score_scale),
        grid=(tiles, kv_count),
        in_specs=[
            pl.BlockSpec((SPAN, 1), lambda t, c: (t, 0)),
            pl.BlockSpec((SPAN, 1), lambda t, c: (t, 0)),
            pl.BlockSpec((1, 1, window), lambda t, c: (t, 0, 0)),
            pl.BlockSpec((SPAN, group_cols), lambda t, c: (t, c)),
            pl.BlockSpec((SPAN, group_cols), lambda t, c: (t, c)),
            pl.BlockSpec((1, window, DH), lambda t, c: (t, 0, c)),
            pl.BlockSpec((1, window, DH), lambda t, c: (t, 0, c)),
        ],
        out_specs=[
            pl.BlockSpec((SPAN, group_cols), lambda t, c: (t, c)),
            pl.BlockSpec((SPAN, group_cols), lambda t, c: (t, c)),
            pl.BlockSpec((1, window, DH), lambda t, c: (t, 0, c)),
            pl.BlockSpec((1, window, DH), lambda t, c: (t, 0, c)),
        ],
        out_shape=[
            jax.ShapeDtypeStruct((local_rows, head_count * DH), jnp.bfloat16),
            jax.ShapeDtypeStruct((local_rows, head_count * DH), jnp.bfloat16),
            jax.ShapeDtypeStruct((tiles, window, kv_cols), jnp.float32),
            jax.ShapeDtypeStruct((tiles, window, kv_cols), jnp.float32),
        ],
    )
    attended, query_grad, key_part, value_part = kernel(
        query_pos, query_start, key_pos, queries, out_grad, key_win, value_win)

    packed = jnp.concatenate([key_part, value_part], axis=2).reshape(
        tiles * window_spans, SPAN, 2 * kv_cols)
    buffer = jnp.zeros((slot_count, SPAN, 2 * kv_cols), jnp.float32)
    buffer = buffer.at[window_slot.reshape(-1)].add(packed)
    summed = lax.psum_scatter(buffer.reshape(total_rows, 2 * kv_cols), "ctx",
                              scatter_dimension=0, tiled=True)
    key_grad = summed[:, :kv_cols].astype(jnp.bfloat16)
    value_grad = summed[:, kv_cols:].astype(jnp.bfloat16)
    return (attended, query_grad, key_grad, value_grad)


def solution(mesh):
    in_specs = (
        P(("groups", "ctx"), "head"),
        P(("groups", "ctx"), "head"),
        P(("groups", "ctx"), "head"),
        P(("groups", "ctx"), "head"),
        P(("groups", "ctx")),
        P("groups"),
    )
    out_specs = (
        P(("groups", "ctx"), "head"),
        P(("groups", "ctx"), "head"),
        P(("groups", "ctx"), "head"),
        P(("groups", "ctx"), "head"),
    )
    return jax.shard_map(local, mesh=mesh, in_specs=in_specs, out_specs=out_specs, check_vma=False)
```

```python
import math

import jax
import jax.numpy as jnp
from jax import lax
from jax.experimental import pallas as pl
from jax.experimental.pallas import tpu as pltpu
from jax.sharding import PartitionSpec as P

DH = 128
SPAN = 64


def attention_kernel(qpos_ref, qstart_ref, kpos_ref, q_ref, do_ref, k_ref, v_ref,
                     out_ref, dq_ref, dk_ref, dv_ref, *, group_size, score_scale):
    qpos = qpos_ref[...]
    qstart = qstart_ref[...]
    kpos = kpos_ref[0]
    visible = (kpos >= qstart) & (kpos <= qpos)
    key_block = k_ref[0]
    value_block = v_ref[0]
    window = key_block.shape[0]
    key_sum = jnp.zeros((window, DH), jnp.float32)
    value_sum = jnp.zeros((window, DH), jnp.float32)
    contract_last = (((1,), (1,)), ((), ()))
    contract_first = (((0,), (0,)), ((), ()))
    for head in range(group_size):
        cols = slice(head * DH, (head + 1) * DH)
        query_head = q_ref[:, cols]
        grad_head = do_ref[:, cols]
        scores = lax.dot_general(query_head, key_block, contract_last,
                                 preferred_element_type=jnp.float32) * score_scale
        masked = jnp.where(visible, scores, -jnp.inf)
        row_max = jnp.max(masked, axis=1, keepdims=True)
        shifted = jnp.where(visible, jnp.exp(masked - row_max), 0.0)
        log_totals = row_max + jnp.log(jnp.sum(shifted, axis=1, keepdims=True))
        weights = jnp.where(visible, jnp.exp(masked - log_totals), 0.0)
        weights_low = weights.astype(jnp.bfloat16)
        attended = jnp.dot(weights_low, value_block,
                           preferred_element_type=jnp.float32).astype(jnp.bfloat16)
        out_ref[:, cols] = attended
        row_dots = jnp.sum(attended.astype(jnp.float32) * grad_head.astype(jnp.float32),
                           axis=1, keepdims=True)
        grad_weights = lax.dot_general(grad_head, value_block, contract_last,
                                       preferred_element_type=jnp.float32)
        grad_scores = (weights * (grad_weights - row_dots)).astype(jnp.bfloat16)
        query_grad = jnp.dot(grad_scores, key_block, preferred_element_type=jnp.float32)
        dq_ref[:, cols] = (query_grad * score_scale).astype(jnp.bfloat16)
        key_sum = key_sum + lax.dot_general(grad_scores, query_head, contract_first,
                                            preferred_element_type=jnp.float32)
        value_sum = value_sum + lax.dot_general(weights_low, grad_head, contract_first,
                                                preferred_element_type=jnp.float32)
    dk_ref[0] = key_sum * score_scale
    dv_ref[0] = value_sum


def local(queries, key_rows, value_rows, out_grad, doc_start, span_order):
    local_rows = queries.shape[0]
    tiles = local_rows // SPAN
    head_count = queries.shape[1] // DH
    kv_count = key_rows.shape[1] // DH
    kv_cols = kv_count * DH
    group_size = head_count // kv_count
    group_cols = group_size * DH
    score_scale = 1.0 / math.sqrt(DH)
    ctx_count = lax.axis_size("ctx")
    my_index = lax.axis_index("ctx")
    total_rows = local_rows * ctx_count
    slot_count = total_rows // SPAN
    reach = total_rows // 4 // SPAN
    window_spans = reach + 1
    window = window_spans * SPAN

    slot_of_span = jnp.zeros((slot_count,), jnp.int32).at[span_order].set(
        jnp.arange(slot_count, dtype=jnp.int32))
    my_spans = lax.dynamic_slice_in_dim(span_order, my_index * tiles, tiles)
    window_span = my_spans[:, None] - reach + jnp.arange(window_spans, dtype=jnp.int32)[None, :]
    window_slot = slot_of_span[jnp.clip(window_span, 0, slot_count - 1)]
    row_in_span = jnp.arange(SPAN, dtype=jnp.int32)
    key_pos = (window_span[:, :, None] * SPAN + row_in_span[None, None, :]).reshape(tiles, 1, window)
    query_pos = (my_spans[:, None] * SPAN + row_in_span[None, :]).reshape(local_rows, 1)
    query_start = doc_start.reshape(local_rows, 1)

    pair = jnp.concatenate([key_rows, value_rows], axis=1)
    pieces = [pair]
    for shift in range(1, ctx_count):
        pieces.append(lax.ppermute(
            pair, "ctx", [(i, (i + shift) % ctx_count) for i in range(ctx_count)]))
    pair_all = jnp.stack(pieces).reshape(ctx_count * tiles, SPAN, 2 * kv_cols)
    window_owner = window_slot // tiles
    window_piece = ((my_index - window_owner) % ctx_count) * tiles + window_slot % tiles
    pair_win = pair_all[window_piece].reshape(tiles, window, 2 * kv_cols)
    key_win = pair_win[:, :, :kv_cols]
    value_win = pair_win[:, :, kv_cols:]

    kernel = pl.pallas_call(
        lambda *refs: attention_kernel(*refs, group_size=group_size, score_scale=score_scale),
        grid=(tiles, kv_count),
        in_specs=[
            pl.BlockSpec((SPAN, 1), lambda t, c: (t, 0)),
            pl.BlockSpec((SPAN, 1), lambda t, c: (t, 0)),
            pl.BlockSpec((1, 1, window), lambda t, c: (t, 0, 0)),
            pl.BlockSpec((SPAN, group_cols), lambda t, c: (t, c)),
            pl.BlockSpec((SPAN, group_cols), lambda t, c: (t, c)),
            pl.BlockSpec((1, window, DH), lambda t, c: (t, 0, c)),
            pl.BlockSpec((1, window, DH), lambda t, c: (t, 0, c)),
        ],
        out_specs=[
            pl.BlockSpec((SPAN, group_cols), lambda t, c: (t, c)),
            pl.BlockSpec((SPAN, group_cols), lambda t, c: (t, c)),
            pl.BlockSpec((1, window, DH), lambda t, c: (t, 0, c)),
            pl.BlockSpec((1, window, DH), lambda t, c: (t, 0, c)),
        ],
        out_shape=[
            jax.ShapeDtypeStruct((local_rows, head_count * DH), jnp.bfloat16),
            jax.ShapeDtypeStruct((local_rows, head_count * DH), jnp.bfloat16),
            jax.ShapeDtypeStruct((tiles, window, kv_cols), jnp.float32),
            jax.ShapeDtypeStruct((tiles, window, kv_cols), jnp.float32),
        ],
    )
    attended, query_grad, key_part, value_part = kernel(
        query_pos, query_start, key_pos, queries, out_grad, key_win, value_win)

    packed = jnp.concatenate([key_part, value_part], axis=2).reshape(
        tiles * window_spans, SPAN, 2 * kv_cols)
    buffer = jnp.zeros((slot_count, SPAN, 2 * kv_cols), jnp.float32)
    buffer = buffer.at[window_slot.reshape(-1)].add(packed)
    blocks = buffer.reshape(ctx_count, local_rows, 2 * kv_cols)
    summed = lax.dynamic_index_in_dim(blocks, my_index, 0, keepdims=False)
    for shift in range(1, ctx_count):
        send = lax.dynamic_index_in_dim(blocks, (my_index + shift) % ctx_count, 0, keepdims=False)
        summed = summed + lax.ppermute(
            send.astype(jnp.bfloat16), "ctx",
            [(i, (i + shift) % ctx_count) for i in range(ctx_count)]).astype(jnp.float32)
    key_grad = summed[:, :kv_cols].astype(jnp.bfloat16)
    value_grad = summed[:, kv_cols:].astype(jnp.bfloat16)
    return (attended, query_grad, key_grad, value_grad)


def solution(mesh):
    in_specs = (
        P(("groups", "ctx"), "head"),
        P(("groups", "ctx"), "head"),
        P(("groups", "ctx"), "head"),
        P(("groups", "ctx"), "head"),
        P(("groups", "ctx")),
        P("groups"),
    )
    out_specs = (
        P(("groups", "ctx"), "head"),
        P(("groups", "ctx"), "head"),
        P(("groups", "ctx"), "head"),
        P(("groups", "ctx"), "head"),
    )
    return jax.shard_map(local, mesh=mesh, in_specs=in_specs, out_specs=out_specs, check_vma=False)
```

```python
import math

import jax
import jax.numpy as jnp
from jax import lax
from jax.experimental import pallas as pl
from jax.experimental.pallas import tpu as pltpu
from jax.sharding import PartitionSpec as P

DH = 128
SPAN = 64
CHUNKS = 2


def attention_kernel(index_ref, qpos_ref, qstart_ref, kpos_ref, q_ref, do_ref, k_ref, v_ref,
                     *rest, group_size, window_spans, tiles, score_scale, aliased):
    if aliased:
        rest = rest[2:]
    out_ref, dq_ref, buf_ref = rest
    tile = pl.program_id(1)
    base = tile * window_spans
    key_block = jnp.concatenate(
        [k_ref[index_ref[base + w]] for w in range(window_spans)], axis=0)
    value_block = jnp.concatenate(
        [v_ref[index_ref[base + w]] for w in range(window_spans)], axis=0)
    query_all = jnp.concatenate(
        [q_ref[:, h * DH:(h + 1) * DH] for h in range(group_size)], axis=0)
    grad_all = jnp.concatenate(
        [do_ref[:, h * DH:(h + 1) * DH] for h in range(group_size)], axis=0)
    kpos = kpos_ref[0]
    visible = (kpos >= qstart_ref[0]) & (kpos <= qpos_ref[0])
    contract_last = (((1,), (1,)), ((), ()))
    contract_first = (((0,), (0,)), ((), ()))
    scores = lax.dot_general(query_all, key_block, contract_last,
                             preferred_element_type=jnp.float32) * score_scale
    masked = jnp.where(visible, scores, -jnp.inf)
    row_max = jnp.max(masked, axis=1, keepdims=True)
    shifted = jnp.where(visible, jnp.exp(masked - row_max), 0.0)
    log_totals = row_max + jnp.log(jnp.sum(shifted, axis=1, keepdims=True))
    weights = jnp.where(visible, jnp.exp(masked - log_totals), 0.0)
    weights_low = weights.astype(jnp.bfloat16)
    attended = jnp.dot(weights_low, value_block,
                       preferred_element_type=jnp.float32).astype(jnp.bfloat16)
    row_dots = jnp.sum(attended.astype(jnp.float32) * grad_all.astype(jnp.float32),
                       axis=1, keepdims=True)
    grad_weights = lax.dot_general(grad_all, value_block, contract_last,
                                   preferred_element_type=jnp.float32)
    grad_scores = (weights * (grad_weights - row_dots)).astype(jnp.bfloat16)
    query_grad = (jnp.dot(grad_scores, key_block, preferred_element_type=jnp.float32)
                  * score_scale).astype(jnp.bfloat16)
    for h in range(group_size):
        out_ref[:, h * DH:(h + 1) * DH] = attended[h * SPAN:(h + 1) * SPAN]
        dq_ref[:, h * DH:(h + 1) * DH] = query_grad[h * SPAN:(h + 1) * SPAN]
    key_sum = lax.dot_general(grad_scores, query_all, contract_first,
                              preferred_element_type=jnp.float32) * score_scale
    value_sum = lax.dot_general(weights_low, grad_all, contract_first,
                                preferred_element_type=jnp.float32)

    @pl.when(tile == 0)
    def _():
        buf_ref[...] = jnp.zeros(buf_ref.shape, buf_ref.dtype)

    slot_base = tiles * window_spans + base
    for w in range(window_spans):
        slot = index_ref[slot_base + w]
        rows = slice(w * SPAN, (w + 1) * SPAN)
        buf_ref[0, slot, :, :DH] += key_sum[rows]
        buf_ref[0, slot, :, DH:] += value_sum[rows]


def local(queries, key_rows, value_rows, out_grad, doc_start, span_order):
    local_rows = queries.shape[0]
    tiles = local_rows // SPAN
    head_count = queries.shape[1] // DH
    kv_count = key_rows.shape[1] // DH
    group_size = head_count // kv_count
    group_cols = group_size * DH
    score_scale = 1.0 / math.sqrt(DH)
    ctx_count = lax.axis_size("ctx")
    my_index = lax.axis_index("ctx")
    total_rows = local_rows * ctx_count
    slot_count = total_rows // SPAN
    reach = total_rows // 4 // SPAN
    window_spans = reach + 1
    window = window_spans * SPAN
    chunks = CHUNKS if kv_count % CHUNKS == 0 else 1
    chunk_heads = kv_count // chunks
    chunk_cols = chunk_heads * DH

    slot_of_span = jnp.zeros((slot_count,), jnp.int32).at[span_order].set(
        jnp.arange(slot_count, dtype=jnp.int32))
    my_spans = lax.dynamic_slice_in_dim(span_order, my_index * tiles, tiles)
    window_span = my_spans[:, None] - reach + jnp.arange(window_spans, dtype=jnp.int32)[None, :]
    window_slot = slot_of_span[jnp.clip(window_span, 0, slot_count - 1)]
    window_owner = window_slot // tiles
    window_piece = ((my_index - window_owner) % ctx_count) * tiles + window_slot % tiles
    index_table = jnp.concatenate([window_piece.reshape(-1), window_slot.reshape(-1)])
    row_in_span = jnp.arange(SPAN, dtype=jnp.int32)
    key_pos = (window_span[:, :, None] * SPAN + row_in_span[None, None, :]).reshape(tiles, 1, window)
    query_pos = my_spans[:, None] * SPAN + row_in_span[None, :]
    query_pos = jnp.tile(query_pos[:, None, :], (1, group_size, 1)).reshape(tiles, group_size * SPAN, 1)
    query_start = jnp.tile(doc_start.reshape(tiles, 1, SPAN), (1, group_size, 1)).reshape(
        tiles, group_size * SPAN, 1)

    def shifted_pairs(shift):
        return [(i, (i + shift) % ctx_count) for i in range(ctx_count)]

    attended = None
    query_grad = None
    key_grads = []
    value_grads = []
    for chunk in range(chunks):
        cols = slice(chunk * chunk_cols, (chunk + 1) * chunk_cols)
        pair = jnp.concatenate([key_rows[:, cols], value_rows[:, cols]], axis=1)
        pieces = [pair]
        for shift in range(1, ctx_count):
            pieces.append(lax.ppermute(pair, "ctx", shifted_pairs(shift)))
        pair_all = jnp.stack(pieces).reshape(ctx_count * tiles, SPAN, 2 * chunk_cols)

        aliased = chunk > 0
        head0 = chunk * chunk_heads
        in_specs = [
            pl.BlockSpec((1, group_size * SPAN, 1), lambda j, t, idx: (t, 0, 0)),
            pl.BlockSpec((1, group_size * SPAN, 1), lambda j, t, idx: (t, 0, 0)),
            pl.BlockSpec((1, 1, window), lambda j, t, idx: (t, 0, 0)),
            pl.BlockSpec((SPAN, group_cols), lambda j, t, idx, h=head0: (t, h + j)),
            pl.BlockSpec((SPAN, group_cols), lambda j, t, idx, h=head0: (t, h + j)),
            pl.BlockSpec((ctx_count * tiles, SPAN, DH), lambda j, t, idx: (0, 0, j)),
            pl.BlockSpec((ctx_count * tiles, SPAN, DH),
                         lambda j, t, idx, n=chunk_heads: (0, 0, n + j)),
        ]
        operands = [index_table, query_pos, query_start, key_pos, queries, out_grad,
                    pair_all, pair_all]
        aliases = {}
        if aliased:
            in_specs += [pl.BlockSpec(memory_space=pl.ANY), pl.BlockSpec(memory_space=pl.ANY)]
            operands += [attended, query_grad]
            aliases = {len(operands) - 2: 0, len(operands) - 1: 1}
        kernel = pl.pallas_call(
            lambda *refs, a=aliased: attention_kernel(
                *refs, group_size=group_size, window_spans=window_spans, tiles=tiles,
                score_scale=score_scale, aliased=a),
            grid_spec=pltpu.PrefetchScalarGridSpec(
                num_scalar_prefetch=1,
                grid=(chunk_heads, tiles),
                in_specs=in_specs,
                out_specs=[
                    pl.BlockSpec((SPAN, group_cols), lambda j, t, idx, h=head0: (t, h + j)),
                    pl.BlockSpec((SPAN, group_cols), lambda j, t, idx, h=head0: (t, h + j)),
                    pl.BlockSpec((1, slot_count, SPAN, 2 * DH), lambda j, t, idx: (j, 0, 0, 0)),
                ],
            ),
            out_shape=[
                jax.ShapeDtypeStruct((local_rows, head_count * DH), jnp.bfloat16),
                jax.ShapeDtypeStruct((local_rows, head_count * DH), jnp.bfloat16),
                jax.ShapeDtypeStruct((chunk_heads, slot_count, SPAN, 2 * DH), jnp.float32),
            ],
            input_output_aliases=aliases,
        )
        attended, query_grad, buffer = kernel(*operands)

        blocks = buffer.reshape(chunk_heads, ctx_count, local_rows, 2 * DH)
        summed = lax.dynamic_index_in_dim(blocks, my_index, 1, keepdims=False)
        for shift in range(1, ctx_count):
            send = lax.dynamic_index_in_dim(blocks, (my_index + shift) % ctx_count, 1,
                                            keepdims=False)
            summed = summed + lax.ppermute(
                send.astype(jnp.bfloat16), "ctx", shifted_pairs(shift)).astype(jnp.float32)
        key_grads.append(summed[:, :, :DH])
        value_grads.append(summed[:, :, DH:])

    def heads_to_cols(parts):
        stacked = jnp.concatenate(parts, axis=0)
        return stacked.transpose(1, 0, 2).reshape(local_rows, kv_count * DH).astype(jnp.bfloat16)

    return (attended, query_grad, heads_to_cols(key_grads), heads_to_cols(value_grads))


def solution(mesh):
    in_specs = (
        P(("groups", "ctx"), "head"),
        P(("groups", "ctx"), "head"),
        P(("groups", "ctx"), "head"),
        P(("groups", "ctx"), "head"),
        P(("groups", "ctx")),
        P("groups"),
    )
    out_specs = (
        P(("groups", "ctx"), "head"),
        P(("groups", "ctx"), "head"),
        P(("groups", "ctx"), "head"),
        P(("groups", "ctx"), "head"),
    )
    return jax.shard_map(local, mesh=mesh, in_specs=in_specs, out_specs=out_specs, check_vma=False)
```

```python
import math

import jax
import jax.numpy as jnp
from jax import lax
from jax.experimental import pallas as pl
from jax.experimental.pallas import tpu as pltpu
from jax.sharding import PartitionSpec as P

DH = 128
SPAN = 64
CHUNKS = 2


def attention_kernel(index_ref, qpos_ref, qstart_ref, kpos_ref, q_ref, do_ref, k_ref, v_ref,
                     *rest, group_size, window_spans, tiles, score_scale, aliased):
    if aliased:
        rest = rest[2:]
    out_ref, dq_ref, buf_ref = rest
    tile = pl.program_id(1)
    base = tile * window_spans
    key_block = jnp.concatenate(
        [k_ref[index_ref[base + w]] for w in range(window_spans)], axis=0)
    value_block = jnp.concatenate(
        [v_ref[index_ref[base + w]] for w in range(window_spans)], axis=0)
    query_all = jnp.concatenate(
        [q_ref[:, h * DH:(h + 1) * DH] for h in range(group_size)], axis=0)
    grad_all = jnp.concatenate(
        [do_ref[:, h * DH:(h + 1) * DH] for h in range(group_size)], axis=0)
    kpos = kpos_ref[0]
    visible = (kpos >= qstart_ref[0]) & (kpos <= qpos_ref[0])
    contract_last = (((1,), (1,)), ((), ()))
    contract_first = (((0,), (0,)), ((), ()))
    scores = lax.dot_general(query_all, key_block, contract_last,
                             preferred_element_type=jnp.float32) * score_scale
    masked = jnp.where(visible, scores, -jnp.inf)
    row_max = jnp.max(masked, axis=1, keepdims=True)
    shifted = jnp.exp(masked - row_max)
    log_totals = row_max + jnp.log(jnp.sum(shifted, axis=1, keepdims=True))
    weights = jnp.exp(masked - log_totals)
    weights_low = weights.astype(jnp.bfloat16)
    attended = jnp.dot(weights_low, value_block,
                       preferred_element_type=jnp.float32).astype(jnp.bfloat16)
    row_dots = jnp.sum(attended.astype(jnp.float32) * grad_all.astype(jnp.float32),
                       axis=1, keepdims=True)
    grad_weights = lax.dot_general(grad_all, value_block, contract_last,
                                   preferred_element_type=jnp.float32)
    grad_scores = (weights * (grad_weights - row_dots)).astype(jnp.bfloat16)
    query_grad = (jnp.dot(grad_scores, key_block, preferred_element_type=jnp.float32)
                  * score_scale).astype(jnp.bfloat16)
    for h in range(group_size):
        out_ref[:, h * DH:(h + 1) * DH] = attended[h * SPAN:(h + 1) * SPAN]
        dq_ref[:, h * DH:(h + 1) * DH] = query_grad[h * SPAN:(h + 1) * SPAN]
    key_sum = lax.dot_general(grad_scores, query_all, contract_first,
                              preferred_element_type=jnp.float32) * score_scale
    value_sum = lax.dot_general(weights_low, grad_all, contract_first,
                                preferred_element_type=jnp.float32)

    @pl.when(tile == 0)
    def _():
        buf_ref[...] = jnp.zeros(buf_ref.shape, buf_ref.dtype)

    slot_base = tiles * window_spans + base
    for w in range(window_spans):
        slot = index_ref[slot_base + w]
        rows = slice(w * SPAN, (w + 1) * SPAN)
        buf_ref[0, slot, :, :DH] += key_sum[rows]
        buf_ref[0, slot, :, DH:] += value_sum[rows]


def local(queries, key_rows, value_rows, out_grad, doc_start, span_order):
    local_rows = queries.shape[0]
    tiles = local_rows // SPAN
    head_count = queries.shape[1] // DH
    kv_count = key_rows.shape[1] // DH
    group_size = head_count // kv_count
    group_cols = group_size * DH
    score_scale = 1.0 / math.sqrt(DH)
    ctx_count = lax.axis_size("ctx")
    my_index = lax.axis_index("ctx")
    total_rows = local_rows * ctx_count
    slot_count = total_rows // SPAN
    reach = total_rows // 4 // SPAN
    window_spans = reach + 1
    window = window_spans * SPAN
    chunks = CHUNKS if kv_count % CHUNKS == 0 else 1
    chunk_heads = kv_count // chunks
    chunk_cols = chunk_heads * DH

    slot_of_span = jnp.zeros((slot_count,), jnp.int32).at[span_order].set(
        jnp.arange(slot_count, dtype=jnp.int32))
    my_spans = lax.dynamic_slice_in_dim(span_order, my_index * tiles, tiles)
    window_span = my_spans[:, None] - reach + jnp.arange(window_spans, dtype=jnp.int32)[None, :]
    window_slot = slot_of_span[jnp.clip(window_span, 0, slot_count - 1)]
    half = ctx_count // 2
    my_half = my_index // half
    my_q = my_index % half
    window_owner = window_slot // tiles
    owner_s = (my_q - window_owner % half) % half
    owner_k = (window_owner // half != my_half).astype(jnp.int32)
    window_piece = (owner_s * 2 + owner_k) * tiles + window_slot % tiles
    index_table = jnp.concatenate([window_piece.reshape(-1), window_slot.reshape(-1)])
    row_in_span = jnp.arange(SPAN, dtype=jnp.int32)
    key_pos = (window_span[:, :, None] * SPAN + row_in_span[None, None, :]).reshape(tiles, 1, window)
    query_pos = my_spans[:, None] * SPAN + row_in_span[None, :]
    query_pos = jnp.tile(query_pos[:, None, :], (1, group_size, 1)).reshape(tiles, group_size * SPAN, 1)
    query_start = jnp.tile(doc_start.reshape(tiles, 1, SPAN), (1, group_size, 1)).reshape(
        tiles, group_size * SPAN, 1)

    def cross_pairs():
        return [(i, i ^ half) for i in range(ctx_count)]

    def half_pairs(shift):
        return [(i, (i // half) * half + (i % half + shift) % half) for i in range(ctx_count)]

    attended = None
    query_grad = None
    key_grads = []
    value_grads = []
    for chunk in range(chunks):
        cols = slice(chunk * chunk_cols, (chunk + 1) * chunk_cols)
        pair = jnp.concatenate([key_rows[:, cols], value_rows[:, cols]], axis=1)
        both = jnp.stack([pair, lax.ppermute(pair, "ctx", cross_pairs())])
        pieces = [both]
        for shift in range(1, half):
            pieces.append(lax.ppermute(both, "ctx", half_pairs(shift)))
        pair_all = jnp.stack(pieces).reshape(ctx_count * tiles, SPAN, 2 * chunk_cols)

        aliased = chunk > 0
        head0 = chunk * chunk_heads
        in_specs = [
            pl.BlockSpec((1, group_size * SPAN, 1), lambda j, t, idx: (t, 0, 0)),
            pl.BlockSpec((1, group_size * SPAN, 1), lambda j, t, idx: (t, 0, 0)),
            pl.BlockSpec((1, 1, window), lambda j, t, idx: (t, 0, 0)),
            pl.BlockSpec((SPAN, group_cols), lambda j, t, idx, h=head0: (t, h + j)),
            pl.BlockSpec((SPAN, group_cols), lambda j, t, idx, h=head0: (t, h + j)),
            pl.BlockSpec((ctx_count * tiles, SPAN, DH), lambda j, t, idx: (0, 0, j)),
            pl.BlockSpec((ctx_count * tiles, SPAN, DH),
                         lambda j, t, idx, n=chunk_heads: (0, 0, n + j)),
        ]
        operands = [index_table, query_pos, query_start, key_pos, queries, out_grad,
                    pair_all, pair_all]
        aliases = {}
        if aliased:
            in_specs += [pl.BlockSpec(memory_space=pl.ANY), pl.BlockSpec(memory_space=pl.ANY)]
            operands += [attended, query_grad]
            aliases = {len(operands) - 2: 0, len(operands) - 1: 1}
        kernel = pl.pallas_call(
            lambda *refs, a=aliased: attention_kernel(
                *refs, group_size=group_size, window_spans=window_spans, tiles=tiles,
                score_scale=score_scale, aliased=a),
            grid_spec=pltpu.PrefetchScalarGridSpec(
                num_scalar_prefetch=1,
                grid=(chunk_heads, tiles),
                in_specs=in_specs,
                out_specs=[
                    pl.BlockSpec((SPAN, group_cols), lambda j, t, idx, h=head0: (t, h + j)),
                    pl.BlockSpec((SPAN, group_cols), lambda j, t, idx, h=head0: (t, h + j)),
                    pl.BlockSpec((1, slot_count, SPAN, 2 * DH), lambda j, t, idx: (j, 0, 0, 0)),
                ],
            ),
            out_shape=[
                jax.ShapeDtypeStruct((local_rows, head_count * DH), jnp.bfloat16),
                jax.ShapeDtypeStruct((local_rows, head_count * DH), jnp.bfloat16),
                jax.ShapeDtypeStruct((chunk_heads, slot_count, SPAN, 2 * DH), jnp.float32),
            ],
            input_output_aliases=aliases,
        )
        attended, query_grad, buffer = kernel(*operands)

        blocks = buffer.reshape(chunk_heads, ctx_count, local_rows, 2 * DH)
        paired = jnp.stack([blocks[:, :half], blocks[:, half:]], axis=1)
        paired = jnp.concatenate([paired, paired[:, ::-1]], axis=2)

        def pack_for(q):
            return lax.dynamic_index_in_dim(paired, my_half * half + q, 2, keepdims=False)

        summed = pack_for(my_q)
        for shift in range(1, half):
            send = pack_for((my_q + shift) % half)
            summed = summed + lax.ppermute(
                send.astype(jnp.bfloat16), "ctx", half_pairs(shift)).astype(jnp.float32)
        summed = summed[:, 0] + lax.ppermute(
            summed[:, 1].astype(jnp.bfloat16), "ctx", cross_pairs()).astype(jnp.float32)
        key_grads.append(summed[:, :, :DH])
        value_grads.append(summed[:, :, DH:])

    def heads_to_cols(parts):
        stacked = jnp.concatenate(parts, axis=0)
        return stacked.transpose(1, 0, 2).reshape(local_rows, kv_count * DH).astype(jnp.bfloat16)

    return (attended, query_grad, heads_to_cols(key_grads), heads_to_cols(value_grads))


def solution(mesh):
    in_specs = (
        P(("groups", "ctx"), "head"),
        P(("groups", "ctx"), "head"),
        P(("groups", "ctx"), "head"),
        P(("groups", "ctx"), "head"),
        P(("groups", "ctx")),
        P("groups"),
    )
    out_specs = (
        P(("groups", "ctx"), "head"),
        P(("groups", "ctx"), "head"),
        P(("groups", "ctx"), "head"),
        P(("groups", "ctx"), "head"),
    )
    return jax.shard_map(local, mesh=mesh, in_specs=in_specs, out_specs=out_specs, check_vma=False)
```

```python
import math

import jax
import jax.numpy as jnp
from jax import lax
from jax.experimental import pallas as pl
from jax.experimental.pallas import tpu as pltpu
from jax.sharding import PartitionSpec as P

DH = 128
SPAN = 64
CHUNKS = 2


def attention_kernel(index_ref, qstart_ref, q_ref, do_ref, k_ref, v_ref,
                     *rest, group_size, window_spans, tiles, score_scale, aliased):
    if aliased:
        rest = rest[2:]
    out_ref, dq_ref, buf_ref = rest
    tile = pl.program_id(1)
    base = tile * window_spans
    key_block = jnp.concatenate(
        [k_ref[index_ref[base + w]] for w in range(window_spans)], axis=0)
    value_block = jnp.concatenate(
        [v_ref[index_ref[base + w]] for w in range(window_spans)], axis=0)
    query_all = jnp.concatenate(
        [q_ref[:, h * DH:(h + 1) * DH] for h in range(group_size)], axis=0)
    grad_all = jnp.concatenate(
        [do_ref[:, h * DH:(h + 1) * DH] for h in range(group_size)], axis=0)
    span = index_ref[2 * tiles * window_spans + tile]
    window = window_spans * SPAN
    row_ids = lax.broadcasted_iota(jnp.int32, (SPAN, window), 0)
    col_ids = lax.broadcasted_iota(jnp.int32, (SPAN, window), 1)
    query_pos = span * SPAN + row_ids
    key_pos = (span - (window_spans - 1)) * SPAN + col_ids
    visible = (key_pos >= qstart_ref[0]) & (key_pos <= query_pos)
    bias = jnp.where(visible, 0.0, -jnp.inf)
    bias = jnp.concatenate([bias] * group_size, axis=0)
    contract_last = (((1,), (1,)), ((), ()))
    contract_first = (((0,), (0,)), ((), ()))
    scores = lax.dot_general(query_all, key_block, contract_last,
                             preferred_element_type=jnp.float32) * score_scale
    masked = scores + bias
    row_max = jnp.max(masked, axis=1, keepdims=True)
    shifted = jnp.exp(masked - row_max)
    log_totals = row_max + jnp.log(jnp.sum(shifted, axis=1, keepdims=True))
    weights = jnp.exp(masked - log_totals)
    weights_low = weights.astype(jnp.bfloat16)
    attended = jnp.dot(weights_low, value_block,
                       preferred_element_type=jnp.float32).astype(jnp.bfloat16)
    row_dots = jnp.sum(attended.astype(jnp.float32) * grad_all.astype(jnp.float32),
                       axis=1, keepdims=True)
    grad_weights = lax.dot_general(grad_all, value_block, contract_last,
                                   preferred_element_type=jnp.float32)
    grad_scores = (weights * (grad_weights - row_dots)).astype(jnp.bfloat16)
    query_grad = (jnp.dot(grad_scores, key_block, preferred_element_type=jnp.float32)
                  * score_scale).astype(jnp.bfloat16)
    for h in range(group_size):
        out_ref[:, h * DH:(h + 1) * DH] = attended[h * SPAN:(h + 1) * SPAN]
        dq_ref[:, h * DH:(h + 1) * DH] = query_grad[h * SPAN:(h + 1) * SPAN]
    key_sum = lax.dot_general(grad_scores, query_all, contract_first,
                              preferred_element_type=jnp.float32) * score_scale
    value_sum = lax.dot_general(weights_low, grad_all, contract_first,
                                preferred_element_type=jnp.float32)

    @pl.when(tile == 0)
    def _():
        buf_ref[...] = jnp.zeros(buf_ref.shape, buf_ref.dtype)

    slot_base = tiles * window_spans + base
    for w in range(window_spans):
        slot = index_ref[slot_base + w]
        rows = slice(w * SPAN, (w + 1) * SPAN)
        buf_ref[0, slot, :, :DH] += key_sum[rows]
        buf_ref[0, slot, :, DH:] += value_sum[rows]


def local(queries, key_rows, value_rows, out_grad, doc_start, span_order):
    local_rows = queries.shape[0]
    tiles = local_rows // SPAN
    head_count = queries.shape[1] // DH
    kv_count = key_rows.shape[1] // DH
    group_size = head_count // kv_count
    group_cols = group_size * DH
    score_scale = 1.0 / math.sqrt(DH)
    ctx_count = lax.axis_size("ctx")
    my_index = lax.axis_index("ctx")
    total_rows = local_rows * ctx_count
    slot_count = total_rows // SPAN
    reach = total_rows // 4 // SPAN
    window_spans = reach + 1
    window = window_spans * SPAN
    chunks = CHUNKS if kv_count % CHUNKS == 0 else 1
    chunk_heads = kv_count // chunks
    chunk_cols = chunk_heads * DH

    my_spans = lax.dynamic_slice_in_dim(span_order, my_index * tiles, tiles)
    window_span = my_spans[:, None] - reach + jnp.arange(window_spans, dtype=jnp.int32)[None, :]
    window_slot = jnp.sum(
        jnp.where(span_order[None, None, :] == window_span[:, :, None],
                  jnp.arange(slot_count, dtype=jnp.int32)[None, None, :], 0), axis=2)
    half = ctx_count // 2
    my_half = my_index // half
    my_q = my_index % half
    window_owner = window_slot // tiles
    owner_s = (my_q - window_owner % half) % half
    owner_k = (window_owner // half != my_half).astype(jnp.int32)
    window_piece = (owner_s * 2 + owner_k) * tiles + window_slot % tiles
    index_table = jnp.concatenate([window_piece.reshape(-1), window_slot.reshape(-1), my_spans])
    query_start = doc_start.reshape(tiles, SPAN, 1)

    def cross_pairs():
        return [(i, i ^ half) for i in range(ctx_count)]

    def half_pairs(shift):
        return [(i, (i // half) * half + (i % half + shift) % half) for i in range(ctx_count)]

    attended = None
    query_grad = None
    key_grads = []
    value_grads = []
    for chunk in range(chunks):
        cols = slice(chunk * chunk_cols, (chunk + 1) * chunk_cols)
        pair = jnp.concatenate([key_rows[:, cols], value_rows[:, cols]], axis=1)
        both = jnp.stack([pair, lax.ppermute(pair, "ctx", cross_pairs())])
        pieces = [both]
        for shift in range(1, half):
            pieces.append(lax.ppermute(both, "ctx", half_pairs(shift)))
        pair_all = jnp.stack(pieces).reshape(ctx_count * tiles, SPAN, 2 * chunk_cols)

        aliased = chunk > 0
        head0 = chunk * chunk_heads
        in_specs = [
            pl.BlockSpec((1, SPAN, 1), lambda j, t, idx: (t, 0, 0)),
            pl.BlockSpec((SPAN, group_cols), lambda j, t, idx, h=head0: (t, h + j)),
            pl.BlockSpec((SPAN, group_cols), lambda j, t, idx, h=head0: (t, h + j)),
            pl.BlockSpec((ctx_count * tiles, SPAN, DH), lambda j, t, idx: (0, 0, j)),
            pl.BlockSpec((ctx_count * tiles, SPAN, DH),
                         lambda j, t, idx, n=chunk_heads: (0, 0, n + j)),
        ]
        operands = [index_table, query_start, queries, out_grad,
                    pair_all, pair_all]
        aliases = {}
        if aliased:
            in_specs += [pl.BlockSpec(memory_space=pl.ANY), pl.BlockSpec(memory_space=pl.ANY)]
            operands += [attended, query_grad]
            aliases = {len(operands) - 2: 0, len(operands) - 1: 1}
        kernel = pl.pallas_call(
            lambda *refs, a=aliased: attention_kernel(
                *refs, group_size=group_size, window_spans=window_spans, tiles=tiles,
                score_scale=score_scale, aliased=a),
            grid_spec=pltpu.PrefetchScalarGridSpec(
                num_scalar_prefetch=1,
                grid=(chunk_heads, tiles),
                in_specs=in_specs,
                out_specs=[
                    pl.BlockSpec((SPAN, group_cols), lambda j, t, idx, h=head0: (t, h + j)),
                    pl.BlockSpec((SPAN, group_cols), lambda j, t, idx, h=head0: (t, h + j)),
                    pl.BlockSpec((1, slot_count, SPAN, 2 * DH), lambda j, t, idx: (j, 0, 0, 0)),
                ],
            ),
            out_shape=[
                jax.ShapeDtypeStruct((local_rows, head_count * DH), jnp.bfloat16),
                jax.ShapeDtypeStruct((local_rows, head_count * DH), jnp.bfloat16),
                jax.ShapeDtypeStruct((chunk_heads, slot_count, SPAN, 2 * DH), jnp.float32),
            ],
            input_output_aliases=aliases,
        )
        attended, query_grad, buffer = kernel(*operands)

        blocks = buffer.reshape(chunk_heads, ctx_count, local_rows, 2 * DH)

        def pack_for(q):
            target = my_half * half + q
            own = lax.dynamic_index_in_dim(blocks, target, 1, keepdims=False)
            other = lax.dynamic_index_in_dim(blocks, target ^ half, 1, keepdims=False)
            return jnp.stack([own, other], axis=1)

        summed = pack_for(my_q)
        for shift in range(1, half):
            send = pack_for((my_q + shift) % half)
            summed = summed + lax.ppermute(
                send.astype(jnp.bfloat16), "ctx", half_pairs(shift)).astype(jnp.float32)
        summed = summed[:, 0] + lax.ppermute(
            summed[:, 1].astype(jnp.bfloat16), "ctx", cross_pairs()).astype(jnp.float32)
        key_grads.append(summed[:, :, :DH])
        value_grads.append(summed[:, :, DH:])

    def heads_to_cols(parts):
        stacked = jnp.concatenate(parts, axis=0)
        return stacked.transpose(1, 0, 2).reshape(local_rows, kv_count * DH).astype(jnp.bfloat16)

    return (attended, query_grad, heads_to_cols(key_grads), heads_to_cols(value_grads))


def solution(mesh):
    in_specs = (
        P(("groups", "ctx"), "head"),
        P(("groups", "ctx"), "head"),
        P(("groups", "ctx"), "head"),
        P(("groups", "ctx"), "head"),
        P(("groups", "ctx")),
        P("groups"),
    )
    out_specs = (
        P(("groups", "ctx"), "head"),
        P(("groups", "ctx"), "head"),
        P(("groups", "ctx"), "head"),
        P(("groups", "ctx"), "head"),
    )
    return jax.shard_map(local, mesh=mesh, in_specs=in_specs, out_specs=out_specs, check_vma=False)
```

```python
import math

import jax
import jax.numpy as jnp
from jax import lax
from jax.experimental import pallas as pl
from jax.experimental.pallas import tpu as pltpu
from jax.sharding import PartitionSpec as P

DH = 128
SPAN = 64
CHUNKS = 2


def attention_kernel(index_ref, qstart_ref, q_ref, do_ref, k_ref, v_ref,
                     *rest, group_size, window_spans, tiles, score_scale, aliased):
    if aliased:
        rest = rest[2:]
    out_ref, dq_ref, buf_ref = rest
    tile = pl.program_id(1)
    base = tile * window_spans
    key_block = jnp.concatenate(
        [k_ref[index_ref[base + w]] for w in range(window_spans)], axis=0)
    value_block = jnp.concatenate(
        [v_ref[index_ref[base + w]] for w in range(window_spans)], axis=0)
    query_all = jnp.concatenate(
        [q_ref[:, h * DH:(h + 1) * DH] for h in range(group_size)], axis=0)
    grad_all = jnp.concatenate(
        [do_ref[:, h * DH:(h + 1) * DH] for h in range(group_size)], axis=0)
    span = index_ref[2 * tiles * window_spans + tile]
    window = window_spans * SPAN
    row_ids = lax.broadcasted_iota(jnp.int32, (SPAN, window), 0)
    col_ids = lax.broadcasted_iota(jnp.int32, (SPAN, window), 1)
    query_pos = span * SPAN + row_ids
    key_pos = (span - (window_spans - 1)) * SPAN + col_ids
    visible = (key_pos >= qstart_ref[0]) & (key_pos <= query_pos)
    bias = jnp.where(visible, 0.0, -jnp.inf)
    bias = jnp.concatenate([bias] * group_size, axis=0)
    contract_last = (((1,), (1,)), ((), ()))
    contract_first = (((0,), (0,)), ((), ()))
    scores = lax.dot_general(query_all, key_block, contract_last,
                             preferred_element_type=jnp.float32) * score_scale
    masked = scores + bias
    row_max = jnp.max(masked, axis=1, keepdims=True)
    shifted = jnp.exp(masked - row_max)
    weights = shifted * (1.0 / jnp.sum(shifted, axis=1, keepdims=True))
    weights_low = weights.astype(jnp.bfloat16)
    attended = jnp.dot(weights_low, value_block,
                       preferred_element_type=jnp.float32).astype(jnp.bfloat16)
    row_dots = jnp.sum(attended.astype(jnp.float32) * grad_all.astype(jnp.float32),
                       axis=1, keepdims=True)
    grad_weights = lax.dot_general(grad_all, value_block, contract_last,
                                   preferred_element_type=jnp.float32)
    grad_scores = (weights * (grad_weights - row_dots)).astype(jnp.bfloat16)
    query_grad = (jnp.dot(grad_scores, key_block, preferred_element_type=jnp.float32)
                  * score_scale).astype(jnp.bfloat16)
    for h in range(group_size):
        out_ref[:, h * DH:(h + 1) * DH] = attended[h * SPAN:(h + 1) * SPAN]
        dq_ref[:, h * DH:(h + 1) * DH] = query_grad[h * SPAN:(h + 1) * SPAN]
    key_sum = lax.dot_general(grad_scores, query_all, contract_first,
                              preferred_element_type=jnp.float32) * score_scale
    value_sum = lax.dot_general(weights_low, grad_all, contract_first,
                                preferred_element_type=jnp.float32)

    @pl.when(tile == 0)
    def _():
        buf_ref[...] = jnp.zeros(buf_ref.shape, buf_ref.dtype)

    slot_base = tiles * window_spans + base
    for w in range(window_spans):
        slot = index_ref[slot_base + w]
        rows = slice(w * SPAN, (w + 1) * SPAN)
        buf_ref[0, slot, :, :DH] += key_sum[rows]
        buf_ref[0, slot, :, DH:] += value_sum[rows]


def local(queries, key_rows, value_rows, out_grad, doc_start, span_order):
    local_rows = queries.shape[0]
    tiles = local_rows // SPAN
    head_count = queries.shape[1] // DH
    kv_count = key_rows.shape[1] // DH
    group_size = head_count // kv_count
    group_cols = group_size * DH
    score_scale = 1.0 / math.sqrt(DH)
    ctx_count = lax.axis_size("ctx")
    my_index = lax.axis_index("ctx")
    total_rows = local_rows * ctx_count
    slot_count = total_rows // SPAN
    reach = total_rows // 4 // SPAN
    window_spans = reach + 1
    window = window_spans * SPAN
    chunks = CHUNKS if kv_count % CHUNKS == 0 else 1
    chunk_heads = kv_count // chunks
    chunk_cols = chunk_heads * DH

    my_spans = lax.dynamic_slice_in_dim(span_order, my_index * tiles, tiles)
    window_span = my_spans[:, None] - reach + jnp.arange(window_spans, dtype=jnp.int32)[None, :]
    window_slot = jnp.sum(
        jnp.where(span_order[None, None, :] == window_span[:, :, None],
                  jnp.arange(slot_count, dtype=jnp.int32)[None, None, :], 0), axis=2)
    half = ctx_count // 2
    my_half = my_index // half
    my_q = my_index % half
    window_owner = window_slot // tiles
    owner_s = (my_q - window_owner % half) % half
    owner_k = (window_owner // half != my_half).astype(jnp.int32)
    window_piece = (owner_s * 2 + owner_k) * tiles + window_slot % tiles
    index_table = jnp.concatenate([window_piece.reshape(-1), window_slot.reshape(-1), my_spans])
    query_start = doc_start.reshape(tiles, SPAN, 1)

    def cross_pairs():
        return [(i, i ^ half) for i in range(ctx_count)]

    def half_pairs(shift):
        return [(i, (i // half) * half + (i % half + shift) % half) for i in range(ctx_count)]

    attended = None
    query_grad = None
    key_grads = []
    value_grads = []
    own = jnp.concatenate([key_rows, value_rows], axis=1)
    partner = lax.ppermute(own, "ctx", cross_pairs())
    own_pieces = [own] + [lax.ppermute(own, "ctx", half_pairs(shift)) for shift in range(1, half)]
    partner_pieces = [partner] + [
        lax.ppermute(partner, "ctx", half_pairs(shift)) for shift in range(1, half)]
    pair_all = jnp.stack([jnp.stack([a, b]) for a, b in zip(own_pieces, partner_pieces)]).reshape(
        ctx_count * tiles, SPAN, 2 * kv_count * DH)
    for chunk in range(chunks):
        aliased = chunk > 0
        head0 = chunk * chunk_heads
        in_specs = [
            pl.BlockSpec((1, SPAN, 1), lambda j, t, idx: (t, 0, 0)),
            pl.BlockSpec((SPAN, group_cols), lambda j, t, idx, h=head0: (t, h + j)),
            pl.BlockSpec((SPAN, group_cols), lambda j, t, idx, h=head0: (t, h + j)),
            pl.BlockSpec((ctx_count * tiles, SPAN, DH), lambda j, t, idx, h=head0: (0, 0, h + j)),
            pl.BlockSpec((ctx_count * tiles, SPAN, DH),
                         lambda j, t, idx, h=kv_count + head0: (0, 0, h + j)),
        ]
        operands = [index_table, query_start, queries, out_grad,
                    pair_all, pair_all]
        aliases = {}
        if aliased:
            in_specs += [pl.BlockSpec(memory_space=pl.ANY), pl.BlockSpec(memory_space=pl.ANY)]
            operands += [attended, query_grad]
            aliases = {len(operands) - 2: 0, len(operands) - 1: 1}
        kernel = pl.pallas_call(
            lambda *refs, a=aliased: attention_kernel(
                *refs, group_size=group_size, window_spans=window_spans, tiles=tiles,
                score_scale=score_scale, aliased=a),
            grid_spec=pltpu.PrefetchScalarGridSpec(
                num_scalar_prefetch=1,
                grid=(chunk_heads, tiles),
                in_specs=in_specs,
                out_specs=[
                    pl.BlockSpec((SPAN, group_cols), lambda j, t, idx, h=head0: (t, h + j)),
                    pl.BlockSpec((SPAN, group_cols), lambda j, t, idx, h=head0: (t, h + j)),
                    pl.BlockSpec((1, slot_count, SPAN, 2 * DH), lambda j, t, idx: (j, 0, 0, 0)),
                ],
            ),
            out_shape=[
                jax.ShapeDtypeStruct((local_rows, head_count * DH), jnp.bfloat16),
                jax.ShapeDtypeStruct((local_rows, head_count * DH), jnp.bfloat16),
                jax.ShapeDtypeStruct((chunk_heads, slot_count, SPAN, 2 * DH), jnp.float32),
            ],
            input_output_aliases=aliases,
        )
        attended, query_grad, buffer = kernel(*operands)

        blocks = buffer.reshape(chunk_heads, ctx_count, local_rows, 2 * DH)

        def pack_for(q):
            target = my_half * half + q
            own = lax.dynamic_index_in_dim(blocks, target, 1, keepdims=False)
            other = lax.dynamic_index_in_dim(blocks, target ^ half, 1, keepdims=False)
            return jnp.stack([own, other], axis=1)

        summed = pack_for(my_q)
        for shift in range(1, half):
            send = pack_for((my_q + shift) % half)
            summed = summed + lax.ppermute(
                send.astype(jnp.bfloat16), "ctx", half_pairs(shift)).astype(jnp.float32)
        summed = summed[:, 0] + lax.ppermute(
            summed[:, 1].astype(jnp.bfloat16), "ctx", cross_pairs()).astype(jnp.float32)
        key_grads.append(summed[:, :, :DH])
        value_grads.append(summed[:, :, DH:])

    def heads_to_cols(parts):
        stacked = jnp.concatenate(parts, axis=0)
        return stacked.transpose(1, 0, 2).reshape(local_rows, kv_count * DH).astype(jnp.bfloat16)

    return (attended, query_grad, heads_to_cols(key_grads), heads_to_cols(value_grads))


def solution(mesh):
    in_specs = (
        P(("groups", "ctx"), "head"),
        P(("groups", "ctx"), "head"),
        P(("groups", "ctx"), "head"),
        P(("groups", "ctx"), "head"),
        P(("groups", "ctx")),
        P("groups"),
    )
    out_specs = (
        P(("groups", "ctx"), "head"),
        P(("groups", "ctx"), "head"),
        P(("groups", "ctx"), "head"),
        P(("groups", "ctx"), "head"),
    )
    return jax.shard_map(local, mesh=mesh, in_specs=in_specs, out_specs=out_specs, check_vma=False)
```

```python
import math

import jax
import jax.numpy as jnp
from jax import lax
from jax.experimental import pallas as pl
from jax.experimental.pallas import tpu as pltpu
from jax.sharding import PartitionSpec as P

DH = 128
SPAN = 64
CHUNKS = 2


def attention_kernel(index_ref, qstart_ref, q_ref, do_ref, k_ref, v_ref,
                     *rest, group_size, window_spans, tiles, half, score_scale, aliased):
    if aliased:
        rest = rest[2:]
    out_ref, dq_ref, own_ref = rest[:3]
    send_refs = rest[3:-1]
    buf_ref = rest[-1]
    tile = pl.program_id(1)
    base = tile * window_spans
    key_block = jnp.concatenate(
        [k_ref[index_ref[base + w]] for w in range(window_spans)], axis=0)
    value_block = jnp.concatenate(
        [v_ref[index_ref[base + w]] for w in range(window_spans)], axis=0)
    query_all = jnp.concatenate(
        [q_ref[:, h * DH:(h + 1) * DH] for h in range(group_size)], axis=0)
    grad_all = jnp.concatenate(
        [do_ref[:, h * DH:(h + 1) * DH] for h in range(group_size)], axis=0)
    span = index_ref[2 * tiles * window_spans + tile]
    window = window_spans * SPAN
    row_ids = lax.broadcasted_iota(jnp.int32, (SPAN, window), 0)
    col_ids = lax.broadcasted_iota(jnp.int32, (SPAN, window), 1)
    query_pos = span * SPAN + row_ids
    key_pos = (span - (window_spans - 1)) * SPAN + col_ids
    visible = (key_pos >= qstart_ref[0]) & (key_pos <= query_pos)
    bias = jnp.where(visible, 0.0, -jnp.inf)
    bias = jnp.concatenate([bias] * group_size, axis=0)
    contract_last = (((1,), (1,)), ((), ()))
    contract_first = (((0,), (0,)), ((), ()))
    scores = lax.dot_general(query_all, key_block, contract_last,
                             preferred_element_type=jnp.float32) * score_scale
    masked = scores + bias
    row_max = jnp.max(masked, axis=1, keepdims=True)
    shifted = jnp.exp(masked - row_max)
    log_totals = row_max + jnp.log(jnp.sum(shifted, axis=1, keepdims=True))
    weights = jnp.exp(masked - log_totals)
    weights_low = weights.astype(jnp.bfloat16)
    attended = jnp.dot(weights_low, value_block,
                       preferred_element_type=jnp.float32).astype(jnp.bfloat16)
    row_dots = jnp.sum(attended.astype(jnp.float32) * grad_all.astype(jnp.float32),
                       axis=1, keepdims=True)
    grad_weights = lax.dot_general(grad_all, value_block, contract_last,
                                   preferred_element_type=jnp.float32)
    grad_scores = (weights * (grad_weights - row_dots)).astype(jnp.bfloat16)
    query_grad = (jnp.dot(grad_scores, key_block, preferred_element_type=jnp.float32)
                  * score_scale).astype(jnp.bfloat16)
    for h in range(group_size):
        out_ref[:, h * DH:(h + 1) * DH] = attended[h * SPAN:(h + 1) * SPAN]
        dq_ref[:, h * DH:(h + 1) * DH] = query_grad[h * SPAN:(h + 1) * SPAN]
    key_sum = lax.dot_general(grad_scores, query_all, contract_first,
                              preferred_element_type=jnp.float32) * score_scale
    value_sum = lax.dot_general(weights_low, grad_all, contract_first,
                                preferred_element_type=jnp.float32)

    @pl.when(tile == 0)
    def _():
        buf_ref[...] = jnp.zeros(buf_ref.shape, buf_ref.dtype)

    slot_base = tiles * window_spans + base
    for w in range(window_spans):
        slot = index_ref[slot_base + w]
        rows = slice(w * SPAN, (w + 1) * SPAN)
        buf_ref[slot, :, :DH] += key_sum[rows]
        buf_ref[slot, :, DH:] += value_sum[rows]

    @pl.when(tile == tiles - 1)
    def _():
        info = 2 * tiles * window_spans + tiles
        my_half = index_ref[info]
        my_q = index_ref[info + 1]
        for shift, ref in enumerate((own_ref,) + tuple(send_refs)):
            target = my_half * half + (my_q + shift) % half
            other = (target + half) % (2 * half)
            for k, device in enumerate((target, other)):
                block = buf_ref[pl.ds(device * tiles, tiles)]
                ref[0, k] = block.astype(ref.dtype)


def local(queries, key_rows, value_rows, out_grad, doc_start, span_order):
    local_rows = queries.shape[0]
    tiles = local_rows // SPAN
    head_count = queries.shape[1] // DH
    kv_count = key_rows.shape[1] // DH
    group_size = head_count // kv_count
    group_cols = group_size * DH
    score_scale = 1.0 / math.sqrt(DH)
    ctx_count = lax.axis_size("ctx")
    my_index = lax.axis_index("ctx")
    total_rows = local_rows * ctx_count
    slot_count = total_rows // SPAN
    reach = total_rows // 4 // SPAN
    window_spans = reach + 1
    window = window_spans * SPAN
    chunks = CHUNKS if kv_count % CHUNKS == 0 else 1
    chunk_heads = kv_count // chunks
    chunk_cols = chunk_heads * DH

    my_spans = lax.dynamic_slice_in_dim(span_order, my_index * tiles, tiles)
    window_span = my_spans[:, None] - reach + jnp.arange(window_spans, dtype=jnp.int32)[None, :]
    window_slot = jnp.sum(
        jnp.where(span_order[None, None, :] == window_span[:, :, None],
                  jnp.arange(slot_count, dtype=jnp.int32)[None, None, :], 0), axis=2)
    half = ctx_count // 2
    my_half = my_index // half
    my_q = my_index % half
    window_owner = window_slot // tiles
    owner_s = (my_q - window_owner % half) % half
    owner_k = (window_owner // half != my_half).astype(jnp.int32)
    window_piece = (owner_s * 2 + owner_k) * tiles + window_slot % tiles
    index_table = jnp.concatenate([window_piece.reshape(-1), window_slot.reshape(-1), my_spans,
                                   jnp.stack([my_half, my_q]).astype(jnp.int32)])
    query_start = doc_start.reshape(tiles, SPAN, 1)

    def cross_pairs():
        return [(i, i ^ half) for i in range(ctx_count)]

    def half_pairs(shift):
        return [(i, (i // half) * half + (i % half + shift) % half) for i in range(ctx_count)]

    attended = None
    query_grad = None
    key_grads = []
    value_grads = []
    for chunk in range(chunks):
        cols = slice(chunk * chunk_cols, (chunk + 1) * chunk_cols)
        pair = jnp.concatenate([key_rows[:, cols], value_rows[:, cols]], axis=1)
        both = jnp.stack([pair, lax.ppermute(pair, "ctx", cross_pairs())])
        pieces = [both]
        for shift in range(1, half):
            pieces.append(lax.ppermute(both, "ctx", half_pairs(shift)))
        pair_all = jnp.stack(pieces).reshape(ctx_count * tiles, SPAN, 2 * chunk_cols)

        aliased = chunk > 0
        head0 = chunk * chunk_heads
        in_specs = [
            pl.BlockSpec((1, SPAN, 1), lambda j, t, idx: (t, 0, 0)),
            pl.BlockSpec((SPAN, group_cols), lambda j, t, idx, h=head0: (t, h + j)),
            pl.BlockSpec((SPAN, group_cols), lambda j, t, idx, h=head0: (t, h + j)),
            pl.BlockSpec((ctx_count * tiles, SPAN, DH), lambda j, t, idx: (0, 0, j)),
            pl.BlockSpec((ctx_count * tiles, SPAN, DH),
                         lambda j, t, idx, n=chunk_heads: (0, 0, n + j)),
        ]
        operands = [index_table, query_start, queries, out_grad,
                    pair_all, pair_all]
        aliases = {}
        if aliased:
            in_specs += [pl.BlockSpec(memory_space=pl.ANY), pl.BlockSpec(memory_space=pl.ANY)]
            operands += [attended, query_grad]
            aliases = {len(operands) - 2: 0, len(operands) - 1: 1}
        kernel = pl.pallas_call(
            lambda *refs, a=aliased: attention_kernel(
                *refs, group_size=group_size, window_spans=window_spans, tiles=tiles,
                half=half, score_scale=score_scale, aliased=a),
            grid_spec=pltpu.PrefetchScalarGridSpec(
                num_scalar_prefetch=1,
                grid=(chunk_heads, tiles),
                in_specs=in_specs,
                out_specs=[
                    pl.BlockSpec((SPAN, group_cols), lambda j, t, idx, h=head0: (t, h + j)),
                    pl.BlockSpec((SPAN, group_cols), lambda j, t, idx, h=head0: (t, h + j)),
                ] + [pl.BlockSpec((1, 2, tiles, SPAN, 2 * DH), lambda j, t, idx: (j, 0, 0, 0, 0))] * half,
                scratch_shapes=[pltpu.VMEM((slot_count, SPAN, 2 * DH), jnp.float32)],
            ),
            out_shape=[
                jax.ShapeDtypeStruct((local_rows, head_count * DH), jnp.bfloat16),
                jax.ShapeDtypeStruct((local_rows, head_count * DH), jnp.bfloat16),
                jax.ShapeDtypeStruct((chunk_heads, 2, tiles, SPAN, 2 * DH), jnp.float32),
            ] + [jax.ShapeDtypeStruct((chunk_heads, 2, tiles, SPAN, 2 * DH), jnp.bfloat16)] * (half - 1),
            input_output_aliases=aliases,
        )
        attended, query_grad, own_pack, *send_packs = kernel(*operands)

        pack_shape = (chunk_heads, 2, local_rows, 2 * DH)
        summed = own_pack.reshape(pack_shape)
        for shift in range(1, half):
            summed = summed + lax.ppermute(
                send_packs[shift - 1].reshape(pack_shape), "ctx",
                half_pairs(shift)).astype(jnp.float32)
        summed = summed[:, 0] + lax.ppermute(
            summed[:, 1].astype(jnp.bfloat16), "ctx", cross_pairs()).astype(jnp.float32)
        key_grads.append(summed[:, :, :DH])
        value_grads.append(summed[:, :, DH:])

    def heads_to_cols(parts):
        stacked = jnp.concatenate(parts, axis=0)
        return stacked.transpose(1, 0, 2).reshape(local_rows, kv_count * DH).astype(jnp.bfloat16)

    return (attended, query_grad, heads_to_cols(key_grads), heads_to_cols(value_grads))


def solution(mesh):
    in_specs = (
        P(("groups", "ctx"), "head"),
        P(("groups", "ctx"), "head"),
        P(("groups", "ctx"), "head"),
        P(("groups", "ctx"), "head"),
        P(("groups", "ctx")),
        P("groups"),
    )
    out_specs = (
        P(("groups", "ctx"), "head"),
        P(("groups", "ctx"), "head"),
        P(("groups", "ctx"), "head"),
        P(("groups", "ctx"), "head"),
    )
    return jax.shard_map(local, mesh=mesh, in_specs=in_specs, out_specs=out_specs, check_vma=False)
```

```python
import math

import jax
import jax.numpy as jnp
from jax import lax
from jax.experimental import pallas as pl
from jax.experimental.pallas import tpu as pltpu
from jax.sharding import PartitionSpec as P

DH = 128
SPAN = 64
CHUNKS = 2


def attention_kernel(index_ref, qstart_ref, q_ref, do_ref,
                     *rest, group_size, window_spans, tiles, half, score_scale, aliased):
    key_refs = rest[:half]
    value_refs = rest[half:2 * half]
    rest = rest[2 * half:]
    if aliased:
        rest = rest[2:]
    out_ref, dq_ref, own_ref = rest[:3]
    send_refs = rest[3:-1]
    buf_ref = rest[-1]
    tile = pl.program_id(1)
    base = tile * window_spans
    info = 2 * tiles * window_spans + tiles

    def window_rows(refs):
        parts = []
        for w in range(window_spans):
            piece = index_ref[base + w]
            row = index_ref[info + 2 + base + w]
            part = refs[0][row]
            for other in range(1, half):
                part = jnp.where(piece == other, refs[other][row], part)
            parts.append(part)
        return jnp.concatenate(parts, axis=0)

    key_block = window_rows(key_refs)
    value_block = window_rows(value_refs)
    query_all = jnp.concatenate(
        [q_ref[:, h * DH:(h + 1) * DH] for h in range(group_size)], axis=0)
    grad_all = jnp.concatenate(
        [do_ref[:, h * DH:(h + 1) * DH] for h in range(group_size)], axis=0)
    span = index_ref[2 * tiles * window_spans + tile]
    window = window_spans * SPAN
    row_ids = lax.broadcasted_iota(jnp.int32, (SPAN, window), 0)
    col_ids = lax.broadcasted_iota(jnp.int32, (SPAN, window), 1)
    query_pos = span * SPAN + row_ids
    key_pos = (span - (window_spans - 1)) * SPAN + col_ids
    visible = (key_pos >= qstart_ref[0]) & (key_pos <= query_pos)
    bias = jnp.where(visible, 0.0, -jnp.inf)
    bias = jnp.concatenate([bias] * group_size, axis=0)
    contract_last = (((1,), (1,)), ((), ()))
    contract_first = (((0,), (0,)), ((), ()))
    scores = lax.dot_general(query_all, key_block, contract_last,
                             preferred_element_type=jnp.float32) * score_scale
    masked = scores + bias
    row_max = jnp.max(masked, axis=1, keepdims=True)
    shifted = jnp.exp(masked - row_max)
    log_totals = row_max + jnp.log(jnp.sum(shifted, axis=1, keepdims=True))
    weights = jnp.exp(masked - log_totals)
    weights_low = weights.astype(jnp.bfloat16)
    attended = jnp.dot(weights_low, value_block,
                       preferred_element_type=jnp.float32).astype(jnp.bfloat16)
    row_dots = jnp.sum(attended.astype(jnp.float32) * grad_all.astype(jnp.float32),
                       axis=1, keepdims=True)
    grad_weights = lax.dot_general(grad_all, value_block, contract_last,
                                   preferred_element_type=jnp.float32)
    grad_scores = (weights * (grad_weights - row_dots)).astype(jnp.bfloat16)
    query_grad = (jnp.dot(grad_scores, key_block, preferred_element_type=jnp.float32)
                  * score_scale).astype(jnp.bfloat16)
    for h in range(group_size):
        out_ref[:, h * DH:(h + 1) * DH] = attended[h * SPAN:(h + 1) * SPAN]
        dq_ref[:, h * DH:(h + 1) * DH] = query_grad[h * SPAN:(h + 1) * SPAN]
    key_sum = lax.dot_general(grad_scores, query_all, contract_first,
                              preferred_element_type=jnp.float32) * score_scale
    value_sum = lax.dot_general(weights_low, grad_all, contract_first,
                                preferred_element_type=jnp.float32)

    @pl.when(tile == 0)
    def _():
        buf_ref[...] = jnp.zeros(buf_ref.shape, buf_ref.dtype)

    slot_base = tiles * window_spans + base
    for w in range(window_spans):
        slot = index_ref[slot_base + w]
        rows = slice(w * SPAN, (w + 1) * SPAN)
        buf_ref[slot, :, :DH] += key_sum[rows]
        buf_ref[slot, :, DH:] += value_sum[rows]

    @pl.when(tile == tiles - 1)
    def _():
        my_half = index_ref[info]
        my_q = index_ref[info + 1]
        for shift, ref in enumerate((own_ref,) + tuple(send_refs)):
            target = my_half * half + (my_q + shift) % half
            other = (target + half) % (2 * half)
            for k, device in enumerate((target, other)):
                block = buf_ref[pl.ds(device * tiles, tiles)]
                ref[k, 0] = block.astype(ref.dtype)


def local(queries, key_rows, value_rows, out_grad, doc_start, span_order):
    local_rows = queries.shape[0]
    tiles = local_rows // SPAN
    head_count = queries.shape[1] // DH
    kv_count = key_rows.shape[1] // DH
    group_size = head_count // kv_count
    group_cols = group_size * DH
    score_scale = 1.0 / math.sqrt(DH)
    ctx_count = lax.axis_size("ctx")
    my_index = lax.axis_index("ctx")
    total_rows = local_rows * ctx_count
    slot_count = total_rows // SPAN
    reach = total_rows // 4 // SPAN
    window_spans = reach + 1
    window = window_spans * SPAN
    chunks = CHUNKS if kv_count % CHUNKS == 0 else 1
    chunk_heads = kv_count // chunks
    chunk_cols = chunk_heads * DH

    my_spans = lax.dynamic_slice_in_dim(span_order, my_index * tiles, tiles)
    window_span = my_spans[:, None] - reach + jnp.arange(window_spans, dtype=jnp.int32)[None, :]
    window_slot = jnp.sum(
        jnp.where(span_order[None, None, :] == window_span[:, :, None],
                  jnp.arange(slot_count, dtype=jnp.int32)[None, None, :], 0), axis=2)
    half = ctx_count // 2
    my_half = my_index // half
    my_q = my_index % half
    window_owner = window_slot // tiles
    owner_s = (my_q - window_owner % half) % half
    owner_k = (window_owner // half != my_half).astype(jnp.int32)
    window_row = owner_k * tiles + window_slot % tiles
    index_table = jnp.concatenate([owner_s.reshape(-1), window_slot.reshape(-1), my_spans,
                                   jnp.stack([my_half, my_q]).astype(jnp.int32),
                                   window_row.reshape(-1)])
    query_start = doc_start.reshape(tiles, SPAN, 1)

    def cross_pairs():
        return [(i, i ^ half) for i in range(ctx_count)]

    def half_pairs(shift):
        return [(i, (i // half) * half + (i % half + shift) % half) for i in range(ctx_count)]

    attended = None
    query_grad = None
    key_grads = []
    value_grads = []
    for chunk in range(chunks):
        cols = slice(chunk * chunk_cols, (chunk + 1) * chunk_cols)
        pair = jnp.concatenate([key_rows[:, cols], value_rows[:, cols]], axis=1)
        both = jnp.stack([pair, lax.ppermute(pair, "ctx", cross_pairs())])
        pieces = [both]
        for shift in range(1, half):
            pieces.append(lax.ppermute(both, "ctx", half_pairs(shift)))
        pieces = [piece.reshape(2 * tiles, SPAN, 2 * chunk_cols) for piece in pieces]

        aliased = chunk > 0
        head0 = chunk * chunk_heads
        in_specs = [
            pl.BlockSpec((1, SPAN, 1), lambda j, t, idx: (t, 0, 0)),
            pl.BlockSpec((SPAN, group_cols), lambda j, t, idx, h=head0: (t, h + j)),
            pl.BlockSpec((SPAN, group_cols), lambda j, t, idx, h=head0: (t, h + j)),
        ] + [pl.BlockSpec((2 * tiles, SPAN, DH), lambda j, t, idx: (0, 0, j))] * half + [
            pl.BlockSpec((2 * tiles, SPAN, DH), lambda j, t, idx, n=chunk_heads: (0, 0, n + j))
        ] * half
        operands = [index_table, query_start, queries, out_grad] + pieces + pieces
        aliases = {}
        if aliased:
            in_specs += [pl.BlockSpec(memory_space=pl.ANY), pl.BlockSpec(memory_space=pl.ANY)]
            operands += [attended, query_grad]
            aliases = {len(operands) - 2: 0, len(operands) - 1: 1}
        kernel = pl.pallas_call(
            lambda *refs, a=aliased: attention_kernel(
                *refs, group_size=group_size, window_spans=window_spans, tiles=tiles,
                half=half, score_scale=score_scale, aliased=a),
            grid_spec=pltpu.PrefetchScalarGridSpec(
                num_scalar_prefetch=1,
                grid=(chunk_heads, tiles),
                in_specs=in_specs,
                out_specs=[
                    pl.BlockSpec((SPAN, group_cols), lambda j, t, idx, h=head0: (t, h + j)),
                    pl.BlockSpec((SPAN, group_cols), lambda j, t, idx, h=head0: (t, h + j)),
                ] + [pl.BlockSpec((2, 1, tiles, SPAN, 2 * DH), lambda j, t, idx: (0, j, 0, 0, 0))] * half,
                scratch_shapes=[pltpu.VMEM((slot_count, SPAN, 2 * DH), jnp.float32)],
            ),
            out_shape=[
                jax.ShapeDtypeStruct((local_rows, head_count * DH), jnp.bfloat16),
                jax.ShapeDtypeStruct((local_rows, head_count * DH), jnp.bfloat16),
                jax.ShapeDtypeStruct((2, chunk_heads, tiles, SPAN, 2 * DH), jnp.float32),
            ] + [jax.ShapeDtypeStruct((2, chunk_heads, tiles, SPAN, 2 * DH), jnp.bfloat16)] * (half - 1),
            input_output_aliases=aliases,
        )
        attended, query_grad, own_pack, *send_packs = kernel(*operands)

        pack_shape = (2, chunk_heads, local_rows, 2 * DH)
        summed = own_pack.reshape(pack_shape)
        for shift in range(1, half):
            summed = summed + lax.ppermute(
                send_packs[shift - 1].reshape(pack_shape), "ctx",
                half_pairs(shift)).astype(jnp.float32)
        summed = summed[0] + lax.ppermute(
            summed[1].astype(jnp.bfloat16), "ctx", cross_pairs()).astype(jnp.float32)
        key_grads.append(summed[:, :, :DH])
        value_grads.append(summed[:, :, DH:])

    def heads_to_cols(parts):
        stacked = jnp.concatenate(parts, axis=0)
        return stacked.transpose(1, 0, 2).reshape(local_rows, kv_count * DH).astype(jnp.bfloat16)

    return (attended, query_grad, heads_to_cols(key_grads), heads_to_cols(value_grads))


def solution(mesh):
    in_specs = (
        P(("groups", "ctx"), "head"),
        P(("groups", "ctx"), "head"),
        P(("groups", "ctx"), "head"),
        P(("groups", "ctx"), "head"),
        P(("groups", "ctx")),
        P("groups"),
    )
    out_specs = (
        P(("groups", "ctx"), "head"),
        P(("groups", "ctx"), "head"),
        P(("groups", "ctx"), "head"),
        P(("groups", "ctx"), "head"),
    )
    return jax.shard_map(local, mesh=mesh, in_specs=in_specs, out_specs=out_specs, check_vma=False)
```

```python
import math

import jax
import jax.numpy as jnp
from jax import lax
from jax.experimental import pallas as pl
from jax.experimental.pallas import tpu as pltpu
from jax.sharding import PartitionSpec as P

DH = 128
SPAN = 64


def attention_kernel(index_ref, qstart_ref, q_ref, do_ref,
                     *rest, group_size, window_spans, tiles, half, score_scale, aliased):
    key_refs = rest[:half]
    value_refs = rest[half:2 * half]
    rest = rest[2 * half:]
    if aliased:
        rest = rest[2:]
    out_ref, dq_ref, own_ref = rest[:3]
    send_refs = rest[3:-1]
    buf_ref = rest[-1]
    tile = pl.program_id(1)
    base = tile * window_spans
    info = 2 * tiles * window_spans + tiles

    def window_rows(refs):
        parts = []
        for w in range(window_spans):
            piece = index_ref[base + w]
            row = index_ref[info + 2 + base + w]
            part = refs[0][row]
            for other in range(1, half):
                part = jnp.where(piece == other, refs[other][row], part)
            parts.append(part)
        return jnp.concatenate(parts, axis=0)

    key_block = window_rows(key_refs)
    value_block = window_rows(value_refs)
    query_all = jnp.concatenate(
        [q_ref[:, h * DH:(h + 1) * DH] for h in range(group_size)], axis=0)
    grad_all = jnp.concatenate(
        [do_ref[:, h * DH:(h + 1) * DH] for h in range(group_size)], axis=0)
    span = index_ref[2 * tiles * window_spans + tile]
    window = window_spans * SPAN
    row_ids = lax.broadcasted_iota(jnp.int32, (SPAN, window), 0)
    col_ids = lax.broadcasted_iota(jnp.int32, (SPAN, window), 1)
    query_pos = span * SPAN + row_ids
    key_pos = (span - (window_spans - 1)) * SPAN + col_ids
    visible = (key_pos >= qstart_ref[0]) & (key_pos <= query_pos)
    bias = jnp.where(visible, 0.0, -jnp.inf)
    bias = jnp.concatenate([bias] * group_size, axis=0)
    contract_last = (((1,), (1,)), ((), ()))
    contract_first = (((0,), (0,)), ((), ()))
    scores = lax.dot_general(query_all, key_block, contract_last,
                             preferred_element_type=jnp.float32) * score_scale
    masked = scores + bias
    row_max = jnp.max(masked, axis=1, keepdims=True)
    shifted = jnp.exp(masked - row_max)
    log_totals = row_max + jnp.log(jnp.sum(shifted, axis=1, keepdims=True))
    weights = jnp.exp(masked - log_totals)
    weights_low = weights.astype(jnp.bfloat16)
    attended = jnp.dot(weights_low, value_block,
                       preferred_element_type=jnp.float32).astype(jnp.bfloat16)
    row_dots = jnp.sum(attended.astype(jnp.float32) * grad_all.astype(jnp.float32),
                       axis=1, keepdims=True)
    grad_weights = lax.dot_general(grad_all, value_block, contract_last,
                                   preferred_element_type=jnp.float32)
    grad_scores = (weights * (grad_weights - row_dots)).astype(jnp.bfloat16)
    query_grad = (jnp.dot(grad_scores, key_block, preferred_element_type=jnp.float32)
                  * score_scale).astype(jnp.bfloat16)
    for h in range(group_size):
        out_ref[:, h * DH:(h + 1) * DH] = attended[h * SPAN:(h + 1) * SPAN]
        dq_ref[:, h * DH:(h + 1) * DH] = query_grad[h * SPAN:(h + 1) * SPAN]
    key_sum = lax.dot_general(grad_scores, query_all, contract_first,
                              preferred_element_type=jnp.float32) * score_scale
    value_sum = lax.dot_general(weights_low, grad_all, contract_first,
                                preferred_element_type=jnp.float32)

    @pl.when(tile == 0)
    def _():
        buf_ref[...] = jnp.zeros(buf_ref.shape, buf_ref.dtype)

    slot_base = tiles * window_spans + base
    for w in range(window_spans):
        slot = index_ref[slot_base + w]
        rows = slice(w * SPAN, (w + 1) * SPAN)
        buf_ref[slot, :, :DH] += key_sum[rows]
        buf_ref[slot, :, DH:] += value_sum[rows]

    @pl.when(tile == tiles - 1)
    def _():
        my_half = index_ref[info]
        my_q = index_ref[info + 1]
        for shift, ref in enumerate((own_ref,) + tuple(send_refs)):
            target = my_half * half + (my_q + shift) % half
            other = (target + half) % (2 * half)
            for k, device in enumerate((target, other)):
                block = buf_ref[pl.ds(device * tiles, tiles)]
                ref[k, 0] = block.astype(ref.dtype)


def local(queries, key_rows, value_rows, out_grad, doc_start, span_order):
    local_rows = queries.shape[0]
    tiles = local_rows // SPAN
    head_count = queries.shape[1] // DH
    kv_count = key_rows.shape[1] // DH
    group_size = head_count // kv_count
    group_cols = group_size * DH
    score_scale = 1.0 / math.sqrt(DH)
    ctx_count = lax.axis_size("ctx")
    my_index = lax.axis_index("ctx")
    total_rows = local_rows * ctx_count
    slot_count = total_rows // SPAN
    reach = total_rows // 4 // SPAN
    window_spans = reach + 1
    window = window_spans * SPAN
    if kv_count >= 4:
        chunk_sizes = [1, kv_count - 2, 1]
    else:
        chunk_sizes = [kv_count]
    chunk_starts = [sum(chunk_sizes[:c]) for c in range(len(chunk_sizes))]

    my_spans = lax.dynamic_slice_in_dim(span_order, my_index * tiles, tiles)
    window_span = my_spans[:, None] - reach + jnp.arange(window_spans, dtype=jnp.int32)[None, :]
    window_slot = jnp.sum(
        jnp.where(span_order[None, None, :] == window_span[:, :, None],
                  jnp.arange(slot_count, dtype=jnp.int32)[None, None, :], 0), axis=2)
    half = ctx_count // 2
    my_half = my_index // half
    my_q = my_index % half
    window_owner = window_slot // tiles
    owner_s = (my_q - window_owner % half) % half
    owner_k = (window_owner // half != my_half).astype(jnp.int32)
    window_row = owner_k * tiles + window_slot % tiles
    index_table = jnp.concatenate([owner_s.reshape(-1), window_slot.reshape(-1), my_spans,
                                   jnp.stack([my_half, my_q]).astype(jnp.int32),
                                   window_row.reshape(-1)])
    query_start = doc_start.reshape(tiles, SPAN, 1)

    def cross_pairs():
        return [(i, i ^ half) for i in range(ctx_count)]

    def half_pairs(shift):
        return [(i, (i // half) * half + (i % half + shift) % half) for i in range(ctx_count)]

    attended = None
    query_grad = None
    key_grads = []
    value_grads = []
    for chunk, (head0, chunk_heads) in enumerate(zip(chunk_starts, chunk_sizes)):
        chunk_cols = chunk_heads * DH
        cols = slice(head0 * DH, (head0 + chunk_heads) * DH)
        pair = jnp.concatenate([key_rows[:, cols], value_rows[:, cols]], axis=1)
        both = jnp.stack([pair, lax.ppermute(pair, "ctx", cross_pairs())])
        pieces = [both]
        for shift in range(1, half):
            pieces.append(lax.ppermute(both, "ctx", half_pairs(shift)))
        pieces = [piece.reshape(2 * tiles, SPAN, 2 * chunk_cols) for piece in pieces]

        aliased = chunk > 0
        in_specs = [
            pl.BlockSpec((1, SPAN, 1), lambda j, t, idx: (t, 0, 0)),
            pl.BlockSpec((SPAN, group_cols), lambda j, t, idx, h=head0: (t, h + j)),
            pl.BlockSpec((SPAN, group_cols), lambda j, t, idx, h=head0: (t, h + j)),
        ] + [pl.BlockSpec((2 * tiles, SPAN, DH), lambda j, t, idx: (0, 0, j))] * half + [
            pl.BlockSpec((2 * tiles, SPAN, DH), lambda j, t, idx, n=chunk_heads: (0, 0, n + j))
        ] * half
        operands = [index_table, query_start, queries, out_grad] + pieces + pieces
        aliases = {}
        if aliased:
            in_specs += [pl.BlockSpec(memory_space=pl.ANY), pl.BlockSpec(memory_space=pl.ANY)]
            operands += [attended, query_grad]
            aliases = {len(operands) - 2: 0, len(operands) - 1: 1}
        kernel = pl.pallas_call(
            lambda *refs, a=aliased: attention_kernel(
                *refs, group_size=group_size, window_spans=window_spans, tiles=tiles,
                half=half, score_scale=score_scale, aliased=a),
            grid_spec=pltpu.PrefetchScalarGridSpec(
                num_scalar_prefetch=1,
                grid=(chunk_heads, tiles),
                in_specs=in_specs,
                out_specs=[
                    pl.BlockSpec((SPAN, group_cols), lambda j, t, idx, h=head0: (t, h + j)),
                    pl.BlockSpec((SPAN, group_cols), lambda j, t, idx, h=head0: (t, h + j)),
                ] + [pl.BlockSpec((2, 1, tiles, SPAN, 2 * DH), lambda j, t, idx: (0, j, 0, 0, 0))] * half,
                scratch_shapes=[pltpu.VMEM((slot_count, SPAN, 2 * DH), jnp.float32)],
            ),
            out_shape=[
                jax.ShapeDtypeStruct((local_rows, head_count * DH), jnp.bfloat16),
                jax.ShapeDtypeStruct((local_rows, head_count * DH), jnp.bfloat16),
                jax.ShapeDtypeStruct((2, chunk_heads, tiles, SPAN, 2 * DH), jnp.float32),
            ] + [jax.ShapeDtypeStruct((2, chunk_heads, tiles, SPAN, 2 * DH), jnp.bfloat16)] * (half - 1),
            input_output_aliases=aliases,
        )
        attended, query_grad, own_pack, *send_packs = kernel(*operands)

        pack_shape = (2, chunk_heads, local_rows, 2 * DH)
        summed = own_pack.reshape(pack_shape)
        for shift in range(1, half):
            summed = summed + lax.ppermute(
                send_packs[shift - 1].reshape(pack_shape), "ctx",
                half_pairs(shift)).astype(jnp.float32)
        summed = summed[0] + lax.ppermute(
            summed[1].astype(jnp.bfloat16), "ctx", cross_pairs()).astype(jnp.float32)
        key_grads.append(summed[:, :, :DH])
        value_grads.append(summed[:, :, DH:])

    def heads_to_cols(parts):
        stacked = jnp.concatenate(parts, axis=0)
        return stacked.transpose(1, 0, 2).reshape(local_rows, kv_count * DH).astype(jnp.bfloat16)

    return (attended, query_grad, heads_to_cols(key_grads), heads_to_cols(value_grads))


def solution(mesh):
    in_specs = (
        P(("groups", "ctx"), "head"),
        P(("groups", "ctx"), "head"),
        P(("groups", "ctx"), "head"),
        P(("groups", "ctx"), "head"),
        P(("groups", "ctx")),
        P("groups"),
    )
    out_specs = (
        P(("groups", "ctx"), "head"),
        P(("groups", "ctx"), "head"),
        P(("groups", "ctx"), "head"),
        P(("groups", "ctx"), "head"),
    )
    return jax.shard_map(local, mesh=mesh, in_specs=in_specs, out_specs=out_specs, check_vma=False)
```

```python
import math

import jax
import jax.numpy as jnp
from jax import lax
from jax.experimental import pallas as pl
from jax.experimental.pallas import tpu as pltpu
from jax.sharding import PartitionSpec as P

DH = 128
SPAN = 64
CHUNKS = 2


def attention_kernel(index_ref, qstart_ref, q_ref, do_ref,
                     *rest, group_size, window_spans, tiles, half, score_scale, aliased):
    key_refs = rest[:half]
    value_refs = rest[half:2 * half]
    rest = rest[2 * half:]
    if aliased:
        rest = rest[2:]
    out_ref, dq_ref, own_ref = rest[:3]
    send_refs = rest[3:-1]
    buf_ref = rest[-1]
    tile = pl.program_id(1)
    base = tile * window_spans
    info = 2 * tiles * window_spans + tiles

    def window_rows(refs):
        parts = []
        for w in range(window_spans):
            piece = index_ref[base + w]
            row = index_ref[info + 2 + base + w]
            part = refs[0][row]
            for other in range(1, half):
                part = jnp.where(piece == other, refs[other][row], part)
            parts.append(part)
        return jnp.concatenate(parts, axis=0)

    key_block = window_rows(key_refs)
    value_block = window_rows(value_refs)
    query_all = jnp.concatenate(
        [q_ref[:, h * DH:(h + 1) * DH] for h in range(group_size)], axis=0)
    grad_all = jnp.concatenate(
        [do_ref[:, h * DH:(h + 1) * DH] for h in range(group_size)], axis=0)
    span = index_ref[2 * tiles * window_spans + tile]
    window = window_spans * SPAN
    row_ids = lax.broadcasted_iota(jnp.int32, (SPAN, window), 0)
    col_ids = lax.broadcasted_iota(jnp.int32, (SPAN, window), 1)
    query_pos = span * SPAN + row_ids
    key_pos = (span - (window_spans - 1)) * SPAN + col_ids
    visible = (key_pos >= qstart_ref[0]) & (key_pos <= query_pos)
    bias = jnp.where(visible, 0.0, -jnp.inf)
    bias = jnp.concatenate([bias] * group_size, axis=0)
    contract_last = (((1,), (1,)), ((), ()))
    contract_first = (((0,), (0,)), ((), ()))
    scores = lax.dot_general(query_all, key_block, contract_last,
                             preferred_element_type=jnp.float32) * score_scale
    masked = scores + bias
    row_max = jnp.max(masked, axis=1, keepdims=True)
    shifted = jnp.exp(masked - row_max)
    log_totals = row_max + jnp.log(jnp.sum(shifted, axis=1, keepdims=True))
    weights = jnp.exp(masked - log_totals)
    weights_low = weights.astype(jnp.bfloat16)
    attended = jnp.dot(weights_low, value_block,
                       preferred_element_type=jnp.float32).astype(jnp.bfloat16)
    row_dots = jnp.sum(attended.astype(jnp.float32) * grad_all.astype(jnp.float32),
                       axis=1, keepdims=True)
    grad_weights = lax.dot_general(grad_all, value_block, contract_last,
                                   preferred_element_type=jnp.float32)
    grad_scores = (weights * (grad_weights - row_dots)).astype(jnp.bfloat16)
    query_grad = (jnp.dot(grad_scores, key_block, preferred_element_type=jnp.float32)
                  * score_scale).astype(jnp.bfloat16)
    for h in range(group_size):
        out_ref[:, h * DH:(h + 1) * DH] = attended[h * SPAN:(h + 1) * SPAN]
        dq_ref[:, h * DH:(h + 1) * DH] = query_grad[h * SPAN:(h + 1) * SPAN]
    key_sum = lax.dot_general(grad_scores, query_all, contract_first,
                              preferred_element_type=jnp.float32) * score_scale
    value_sum = lax.dot_general(weights_low, grad_all, contract_first,
                                preferred_element_type=jnp.float32)

    @pl.when(tile == 0)
    def _():
        buf_ref[...] = jnp.zeros(buf_ref.shape, buf_ref.dtype)

    slot_base = tiles * window_spans + base
    for w in range(window_spans):
        slot = index_ref[slot_base + w]
        rows = slice(w * SPAN, (w + 1) * SPAN)
        buf_ref[slot, :, :DH] += key_sum[rows]
        buf_ref[slot, :, DH:] += value_sum[rows]

    @pl.when(tile == tiles - 1)
    def _():
        my_half = index_ref[info]
        my_q = index_ref[info + 1]
        for shift, ref in enumerate((own_ref,) + tuple(send_refs)):
            target = my_half * half + (my_q + shift) % half
            other = (target + half) % (2 * half)
            for k, device in enumerate((target, other)):
                block = buf_ref[pl.ds(device * tiles, tiles)]
                ref[k, 0] = block.astype(ref.dtype)


def local(queries, key_rows, value_rows, out_grad, doc_start, span_order):
    local_rows = queries.shape[0]
    tiles = local_rows // SPAN
    head_count = queries.shape[1] // DH
    kv_count = key_rows.shape[1] // DH
    group_size = head_count // kv_count
    group_cols = group_size * DH
    score_scale = 1.0 / math.sqrt(DH)
    ctx_count = lax.axis_size("ctx")
    my_index = lax.axis_index("ctx")
    total_rows = local_rows * ctx_count
    slot_count = total_rows // SPAN
    reach = total_rows // 4 // SPAN
    window_spans = reach + 1
    window = window_spans * SPAN
    chunks = CHUNKS if kv_count % CHUNKS == 0 else 1
    chunk_heads = kv_count // chunks
    chunk_cols = chunk_heads * DH

    my_spans = lax.dynamic_slice_in_dim(span_order, my_index * tiles, tiles)
    window_span = my_spans[:, None] - reach + jnp.arange(window_spans, dtype=jnp.int32)[None, :]
    window_slot = jnp.sum(
        jnp.where(span_order[None, None, :] == window_span[:, :, None],
                  jnp.arange(slot_count, dtype=jnp.int32)[None, None, :], 0), axis=2)
    half = ctx_count // 2
    my_half = my_index // half
    my_q = my_index % half
    window_owner = window_slot // tiles
    owner_s = (my_q - window_owner % half) % half
    owner_k = (window_owner // half != my_half).astype(jnp.int32)
    window_row = owner_k * tiles + window_slot % tiles
    index_table = jnp.concatenate([owner_s.reshape(-1), window_slot.reshape(-1), my_spans,
                                   jnp.stack([my_half, my_q]).astype(jnp.int32),
                                   window_row.reshape(-1)])
    query_start = doc_start.reshape(tiles, SPAN, 1)

    def cross_pairs():
        return [(i, i ^ half) for i in range(ctx_count)]

    def half_pairs(shift):
        return [(i, (i // half) * half + (i % half + shift) % half) for i in range(ctx_count)]

    attended = None
    query_grad = None
    key_grads = []
    value_grads = []
    chunk_boths = []
    for chunk in range(chunks):
        cols = slice(chunk * chunk_cols, (chunk + 1) * chunk_cols)
        pair = jnp.concatenate([key_rows[:, cols], value_rows[:, cols]], axis=1)
        chunk_boths.append(jnp.stack([pair, lax.ppermute(pair, "ctx", cross_pairs())]))
    gathered = []
    for chunk in range(chunks):
        both = chunk_boths[chunk]
        pieces = [both]
        for shift in range(1, half):
            pieces.append(lax.ppermute(both, "ctx", half_pairs(shift)))
        gathered.append([piece.reshape(2 * tiles, SPAN, 2 * chunk_cols) for piece in pieces])
        if chunk + 1 < chunks:
            gathered[chunk], chunk_boths[chunk + 1] = lax.optimization_barrier(
                (gathered[chunk], chunk_boths[chunk + 1]))

    for chunk in range(chunks):
        pieces = gathered[chunk]
        aliased = chunk > 0
        head0 = chunk * chunk_heads
        in_specs = [
            pl.BlockSpec((1, SPAN, 1), lambda j, t, idx: (t, 0, 0)),
            pl.BlockSpec((SPAN, group_cols), lambda j, t, idx, h=head0: (t, h + j)),
            pl.BlockSpec((SPAN, group_cols), lambda j, t, idx, h=head0: (t, h + j)),
        ] + [pl.BlockSpec((2 * tiles, SPAN, DH), lambda j, t, idx: (0, 0, j))] * half + [
            pl.BlockSpec((2 * tiles, SPAN, DH), lambda j, t, idx, n=chunk_heads: (0, 0, n + j))
        ] * half
        operands = [index_table, query_start, queries, out_grad] + pieces + pieces
        aliases = {}
        if aliased:
            in_specs += [pl.BlockSpec(memory_space=pl.ANY), pl.BlockSpec(memory_space=pl.ANY)]
            operands += [attended, query_grad]
            aliases = {len(operands) - 2: 0, len(operands) - 1: 1}
        kernel = pl.pallas_call(
            lambda *refs, a=aliased: attention_kernel(
                *refs, group_size=group_size, window_spans=window_spans, tiles=tiles,
                half=half, score_scale=score_scale, aliased=a),
            grid_spec=pltpu.PrefetchScalarGridSpec(
                num_scalar_prefetch=1,
                grid=(chunk_heads, tiles),
                in_specs=in_specs,
                out_specs=[
                    pl.BlockSpec((SPAN, group_cols), lambda j, t, idx, h=head0: (t, h + j)),
                    pl.BlockSpec((SPAN, group_cols), lambda j, t, idx, h=head0: (t, h + j)),
                ] + [pl.BlockSpec((2, 1, tiles, SPAN, 2 * DH), lambda j, t, idx: (0, j, 0, 0, 0))] * half,
                scratch_shapes=[pltpu.VMEM((slot_count, SPAN, 2 * DH), jnp.float32)],
            ),
            out_shape=[
                jax.ShapeDtypeStruct((local_rows, head_count * DH), jnp.bfloat16),
                jax.ShapeDtypeStruct((local_rows, head_count * DH), jnp.bfloat16),
                jax.ShapeDtypeStruct((2, chunk_heads, tiles, SPAN, 2 * DH), jnp.float32),
            ] + [jax.ShapeDtypeStruct((2, chunk_heads, tiles, SPAN, 2 * DH), jnp.bfloat16)] * (half - 1),
            input_output_aliases=aliases,
        )
        attended, query_grad, own_pack, *send_packs = kernel(*operands)

        pack_shape = (2, chunk_heads, local_rows, 2 * DH)
        summed = own_pack.reshape(pack_shape)
        for shift in range(1, half):
            summed = summed + lax.ppermute(
                send_packs[shift - 1].reshape(pack_shape), "ctx",
                half_pairs(shift)).astype(jnp.float32)
        summed = summed[0] + lax.ppermute(
            summed[1].astype(jnp.bfloat16), "ctx", cross_pairs()).astype(jnp.float32)
        key_grads.append(summed[:, :, :DH])
        value_grads.append(summed[:, :, DH:])

    def heads_to_cols(parts):
        stacked = jnp.concatenate(parts, axis=0)
        return stacked.transpose(1, 0, 2).reshape(local_rows, kv_count * DH).astype(jnp.bfloat16)

    return (attended, query_grad, heads_to_cols(key_grads), heads_to_cols(value_grads))


def solution(mesh):
    in_specs = (
        P(("groups", "ctx"), "head"),
        P(("groups", "ctx"), "head"),
        P(("groups", "ctx"), "head"),
        P(("groups", "ctx"), "head"),
        P(("groups", "ctx")),
        P("groups"),
    )
    out_specs = (
        P(("groups", "ctx"), "head"),
        P(("groups", "ctx"), "head"),
        P(("groups", "ctx"), "head"),
        P(("groups", "ctx"), "head"),
    )
    return jax.shard_map(local, mesh=mesh, in_specs=in_specs, out_specs=out_specs, check_vma=False)
```

```python
import math

import jax
import jax.numpy as jnp
from jax import lax
from jax.experimental import pallas as pl
from jax.experimental.pallas import tpu as pltpu
from jax.sharding import PartitionSpec as P

DH = 128
SPAN = 64
CHUNKS = 2


def attention_kernel(index_ref, qstart_ref, q_ref, do_ref,
                     *rest, group_size, window_spans, tiles, half, score_scale, aliased):
    key_refs = rest[:half]
    value_refs = rest[half:2 * half]
    rest = rest[2 * half:]
    if aliased:
        rest = rest[2:]
    out_ref, dq_ref, own_ref = rest[:3]
    send_refs = rest[3:-1]
    buf_ref = rest[-1]
    info = 2 * tiles * window_spans + tiles
    buf_ref[...] = jnp.zeros(buf_ref.shape, buf_ref.dtype)
    for tile in range(tiles):
        rows = slice(tile * SPAN, (tile + 1) * SPAN)
        base = tile * window_spans

        def window_rows(refs):
            parts = []
            for w in range(window_spans):
                piece = index_ref[base + w]
                row = index_ref[info + 2 + base + w]
                part = refs[0][row]
                for other in range(1, half):
                    part = jnp.where(piece == other, refs[other][row], part)
                parts.append(part)
            return jnp.concatenate(parts, axis=0)

        key_block = window_rows(key_refs)
        value_block = window_rows(value_refs)
        query_all = jnp.concatenate(
            [q_ref[rows, h * DH:(h + 1) * DH] for h in range(group_size)], axis=0)
        grad_all = jnp.concatenate(
            [do_ref[rows, h * DH:(h + 1) * DH] for h in range(group_size)], axis=0)
        span = index_ref[2 * tiles * window_spans + tile]
        window = window_spans * SPAN
        row_ids = lax.broadcasted_iota(jnp.int32, (SPAN, window), 0)
        col_ids = lax.broadcasted_iota(jnp.int32, (SPAN, window), 1)
        query_pos = span * SPAN + row_ids
        key_pos = (span - (window_spans - 1)) * SPAN + col_ids
        visible = (key_pos >= qstart_ref[tile]) & (key_pos <= query_pos)
        bias = jnp.where(visible, 0.0, -jnp.inf)
        bias = jnp.concatenate([bias] * group_size, axis=0)
        contract_last = (((1,), (1,)), ((), ()))
        contract_first = (((0,), (0,)), ((), ()))
        scores = lax.dot_general(query_all, key_block, contract_last,
                                 preferred_element_type=jnp.float32) * score_scale
        masked = scores + bias
        row_max = jnp.max(masked, axis=1, keepdims=True)
        shifted = jnp.exp(masked - row_max)
        log_totals = row_max + jnp.log(jnp.sum(shifted, axis=1, keepdims=True))
        weights = jnp.exp(masked - log_totals)
        weights_low = weights.astype(jnp.bfloat16)
        attended = jnp.dot(weights_low, value_block,
                           preferred_element_type=jnp.float32).astype(jnp.bfloat16)
        row_dots = jnp.sum(attended.astype(jnp.float32) * grad_all.astype(jnp.float32),
                           axis=1, keepdims=True)
        grad_weights = lax.dot_general(grad_all, value_block, contract_last,
                                       preferred_element_type=jnp.float32)
        grad_scores = (weights * (grad_weights - row_dots)).astype(jnp.bfloat16)
        query_grad = (jnp.dot(grad_scores, key_block, preferred_element_type=jnp.float32)
                      * score_scale).astype(jnp.bfloat16)
        for h in range(group_size):
            out_ref[rows, h * DH:(h + 1) * DH] = attended[h * SPAN:(h + 1) * SPAN]
            dq_ref[rows, h * DH:(h + 1) * DH] = query_grad[h * SPAN:(h + 1) * SPAN]
        key_sum = lax.dot_general(grad_scores, query_all, contract_first,
                                  preferred_element_type=jnp.float32) * score_scale
        value_sum = lax.dot_general(weights_low, grad_all, contract_first,
                                    preferred_element_type=jnp.float32)

        slot_base = tiles * window_spans + base
        for w in range(window_spans):
            slot = index_ref[slot_base + w]
            part = slice(w * SPAN, (w + 1) * SPAN)
            buf_ref[slot, :, :DH] += key_sum[part]
            buf_ref[slot, :, DH:] += value_sum[part]

    my_half = index_ref[info]
    my_q = index_ref[info + 1]
    for shift, ref in enumerate((own_ref,) + tuple(send_refs)):
        target = my_half * half + (my_q + shift) % half
        other = (target + half) % (2 * half)
        for k, device in enumerate((target, other)):
            block = buf_ref[pl.ds(device * tiles, tiles)]
            ref[k, 0] = block.astype(ref.dtype)


def local(queries, key_rows, value_rows, out_grad, doc_start, span_order):
    local_rows = queries.shape[0]
    tiles = local_rows // SPAN
    head_count = queries.shape[1] // DH
    kv_count = key_rows.shape[1] // DH
    group_size = head_count // kv_count
    group_cols = group_size * DH
    score_scale = 1.0 / math.sqrt(DH)
    ctx_count = lax.axis_size("ctx")
    my_index = lax.axis_index("ctx")
    total_rows = local_rows * ctx_count
    slot_count = total_rows // SPAN
    reach = total_rows // 4 // SPAN
    window_spans = reach + 1
    window = window_spans * SPAN
    chunks = CHUNKS if kv_count % CHUNKS == 0 else 1
    chunk_heads = kv_count // chunks
    chunk_cols = chunk_heads * DH

    my_spans = lax.dynamic_slice_in_dim(span_order, my_index * tiles, tiles)
    window_span = my_spans[:, None] - reach + jnp.arange(window_spans, dtype=jnp.int32)[None, :]
    window_slot = jnp.sum(
        jnp.where(span_order[None, None, :] == window_span[:, :, None],
                  jnp.arange(slot_count, dtype=jnp.int32)[None, None, :], 0), axis=2)
    half = ctx_count // 2
    my_half = my_index // half
    my_q = my_index % half
    window_owner = window_slot // tiles
    owner_s = (my_q - window_owner % half) % half
    owner_k = (window_owner // half != my_half).astype(jnp.int32)
    window_row = owner_k * tiles + window_slot % tiles
    index_table = jnp.concatenate([owner_s.reshape(-1), window_slot.reshape(-1), my_spans,
                                   jnp.stack([my_half, my_q]).astype(jnp.int32),
                                   window_row.reshape(-1)])
    query_start = doc_start.reshape(tiles, SPAN, 1)

    def cross_pairs():
        return [(i, i ^ half) for i in range(ctx_count)]

    def half_pairs(shift):
        return [(i, (i // half) * half + (i % half + shift) % half) for i in range(ctx_count)]

    attended = None
    query_grad = None
    key_grads = []
    value_grads = []
    for chunk in range(chunks):
        cols = slice(chunk * chunk_cols, (chunk + 1) * chunk_cols)
        pair = jnp.concatenate([key_rows[:, cols], value_rows[:, cols]], axis=1)
        both = jnp.stack([pair, lax.ppermute(pair, "ctx", cross_pairs())])
        pieces = [both]
        for shift in range(1, half):
            pieces.append(lax.ppermute(both, "ctx", half_pairs(shift)))
        pieces = [piece.reshape(2 * tiles, SPAN, 2 * chunk_cols) for piece in pieces]

        aliased = chunk > 0
        head0 = chunk * chunk_heads
        in_specs = [
            pl.BlockSpec((tiles, SPAN, 1), lambda j, idx: (0, 0, 0)),
            pl.BlockSpec((local_rows, group_cols), lambda j, idx, h=head0: (0, h + j)),
            pl.BlockSpec((local_rows, group_cols), lambda j, idx, h=head0: (0, h + j)),
        ] + [pl.BlockSpec((2 * tiles, SPAN, DH), lambda j, idx: (0, 0, j))] * half + [
            pl.BlockSpec((2 * tiles, SPAN, DH), lambda j, idx, n=chunk_heads: (0, 0, n + j))
        ] * half
        operands = [index_table, query_start, queries, out_grad] + pieces + pieces
        aliases = {}
        if aliased:
            in_specs += [pl.BlockSpec(memory_space=pl.ANY), pl.BlockSpec(memory_space=pl.ANY)]
            operands += [attended, query_grad]
            aliases = {len(operands) - 2: 0, len(operands) - 1: 1}
        kernel = pl.pallas_call(
            lambda *refs, a=aliased: attention_kernel(
                *refs, group_size=group_size, window_spans=window_spans, tiles=tiles,
                half=half, score_scale=score_scale, aliased=a),
            grid_spec=pltpu.PrefetchScalarGridSpec(
                num_scalar_prefetch=1,
                grid=(chunk_heads,),
                in_specs=in_specs,
                out_specs=[
                    pl.BlockSpec((local_rows, group_cols), lambda j, idx, h=head0: (0, h + j)),
                    pl.BlockSpec((local_rows, group_cols), lambda j, idx, h=head0: (0, h + j)),
                ] + [pl.BlockSpec((2, 1, tiles, SPAN, 2 * DH), lambda j, idx: (0, j, 0, 0, 0))] * half,
                scratch_shapes=[pltpu.VMEM((slot_count, SPAN, 2 * DH), jnp.float32)],
            ),
            out_shape=[
                jax.ShapeDtypeStruct((local_rows, head_count * DH), jnp.bfloat16),
                jax.ShapeDtypeStruct((local_rows, head_count * DH), jnp.bfloat16),
                jax.ShapeDtypeStruct((2, chunk_heads, tiles, SPAN, 2 * DH), jnp.float32),
            ] + [jax.ShapeDtypeStruct((2, chunk_heads, tiles, SPAN, 2 * DH), jnp.bfloat16)] * (half - 1),
            input_output_aliases=aliases,
        )
        attended, query_grad, own_pack, *send_packs = kernel(*operands)

        pack_shape = (2, chunk_heads, local_rows, 2 * DH)
        summed = own_pack.reshape(pack_shape)
        for shift in range(1, half):
            summed = summed + lax.ppermute(
                send_packs[shift - 1].reshape(pack_shape), "ctx",
                half_pairs(shift)).astype(jnp.float32)
        summed = summed[0] + lax.ppermute(
            summed[1].astype(jnp.bfloat16), "ctx", cross_pairs()).astype(jnp.float32)
        key_grads.append(summed[:, :, :DH])
        value_grads.append(summed[:, :, DH:])

    def heads_to_cols(parts):
        stacked = jnp.concatenate(parts, axis=0)
        return stacked.transpose(1, 0, 2).reshape(local_rows, kv_count * DH).astype(jnp.bfloat16)

    return (attended, query_grad, heads_to_cols(key_grads), heads_to_cols(value_grads))


def solution(mesh):
    in_specs = (
        P(("groups", "ctx"), "head"),
        P(("groups", "ctx"), "head"),
        P(("groups", "ctx"), "head"),
        P(("groups", "ctx"), "head"),
        P(("groups", "ctx")),
        P("groups"),
    )
    out_specs = (
        P(("groups", "ctx"), "head"),
        P(("groups", "ctx"), "head"),
        P(("groups", "ctx"), "head"),
        P(("groups", "ctx"), "head"),
    )
    return jax.shard_map(local, mesh=mesh, in_specs=in_specs, out_specs=out_specs, check_vma=False)
```

```python
import math

import jax
import jax.numpy as jnp
from jax import lax
from jax.experimental import pallas as pl
from jax.experimental.pallas import tpu as pltpu
from jax.sharding import PartitionSpec as P

DH = 128
SPAN = 64
CHUNKS = 2


def attention_kernel(index_ref, qstart_ref, q_ref, do_ref,
                     *rest, group_size, window_spans, tiles, half, score_scale, aliased):
    key_refs = rest[:2 * half]
    value_refs = rest[2 * half:4 * half]
    rest = rest[4 * half:]
    if aliased:
        rest = rest[2:]
    out_ref, dq_ref, own_ref = rest[:3]
    send_refs = rest[3:-1]
    buf_ref = rest[-1]
    info = 2 * tiles * window_spans + tiles
    buf_ref[...] = jnp.zeros(buf_ref.shape, buf_ref.dtype)
    for tile in range(tiles):
        rows = slice(tile * SPAN, (tile + 1) * SPAN)
        base = tile * window_spans

        def window_rows(refs):
            parts = []
            for w in range(window_spans):
                piece = index_ref[base + w]
                row = index_ref[info + 2 + base + w]
                part = refs[0][row]
                for other in range(1, len(refs)):
                    part = jnp.where(piece == other, refs[other][row], part)
                parts.append(part)
            return jnp.concatenate(parts, axis=0)

        key_block = window_rows(key_refs)
        value_block = window_rows(value_refs)
        query_all = jnp.concatenate(
            [q_ref[rows, h * DH:(h + 1) * DH] for h in range(group_size)], axis=0)
        grad_all = jnp.concatenate(
            [do_ref[rows, h * DH:(h + 1) * DH] for h in range(group_size)], axis=0)
        span = index_ref[2 * tiles * window_spans + tile]
        window = window_spans * SPAN
        row_ids = lax.broadcasted_iota(jnp.int32, (SPAN, window), 0)
        col_ids = lax.broadcasted_iota(jnp.int32, (SPAN, window), 1)
        query_pos = span * SPAN + row_ids
        key_pos = (span - (window_spans - 1)) * SPAN + col_ids
        visible = (key_pos >= qstart_ref[tile]) & (key_pos <= query_pos)
        bias = jnp.where(visible, 0.0, -jnp.inf)
        bias = jnp.concatenate([bias] * group_size, axis=0)
        contract_last = (((1,), (1,)), ((), ()))
        contract_first = (((0,), (0,)), ((), ()))
        scores = lax.dot_general(query_all, key_block, contract_last,
                                 preferred_element_type=jnp.float32) * score_scale
        masked = scores + bias
        row_max = jnp.max(masked, axis=1, keepdims=True)
        shifted = jnp.exp(masked - row_max)
        log_totals = row_max + jnp.log(jnp.sum(shifted, axis=1, keepdims=True))
        weights = jnp.exp(masked - log_totals)
        weights_low = weights.astype(jnp.bfloat16)
        attended = jnp.dot(weights_low, value_block,
                           preferred_element_type=jnp.float32).astype(jnp.bfloat16)
        row_dots = jnp.sum(attended.astype(jnp.float32) * grad_all.astype(jnp.float32),
                           axis=1, keepdims=True)
        grad_weights = lax.dot_general(grad_all, value_block, contract_last,
                                       preferred_element_type=jnp.float32)
        grad_scores = (weights * (grad_weights - row_dots)).astype(jnp.bfloat16)
        query_grad = (jnp.dot(grad_scores, key_block, preferred_element_type=jnp.float32)
                      * score_scale).astype(jnp.bfloat16)
        for h in range(group_size):
            out_ref[rows, h * DH:(h + 1) * DH] = attended[h * SPAN:(h + 1) * SPAN]
            dq_ref[rows, h * DH:(h + 1) * DH] = query_grad[h * SPAN:(h + 1) * SPAN]
        key_sum = lax.dot_general(grad_scores, query_all, contract_first,
                                  preferred_element_type=jnp.float32) * score_scale
        value_sum = lax.dot_general(weights_low, grad_all, contract_first,
                                    preferred_element_type=jnp.float32)

        slot_base = tiles * window_spans + base
        for w in range(window_spans):
            slot = index_ref[slot_base + w]
            part = slice(w * SPAN, (w + 1) * SPAN)
            buf_ref[slot, :, :DH] += key_sum[part]
            buf_ref[slot, :, DH:] += value_sum[part]

    my_half = index_ref[info]
    my_q = index_ref[info + 1]
    for shift, ref in enumerate((own_ref,) + tuple(send_refs)):
        target = my_half * half + (my_q + shift) % half
        other = (target + half) % (2 * half)
        for k, device in enumerate((target, other)):
            block = buf_ref[pl.ds(device * tiles, tiles)]
            ref[k, 0] = block.astype(ref.dtype)


def local(queries, key_rows, value_rows, out_grad, doc_start, span_order):
    local_rows = queries.shape[0]
    tiles = local_rows // SPAN
    head_count = queries.shape[1] // DH
    kv_count = key_rows.shape[1] // DH
    group_size = head_count // kv_count
    group_cols = group_size * DH
    score_scale = 1.0 / math.sqrt(DH)
    ctx_count = lax.axis_size("ctx")
    my_index = lax.axis_index("ctx")
    total_rows = local_rows * ctx_count
    slot_count = total_rows // SPAN
    reach = total_rows // 4 // SPAN
    window_spans = reach + 1
    window = window_spans * SPAN
    chunks = CHUNKS if kv_count % CHUNKS == 0 else 1
    chunk_heads = kv_count // chunks
    chunk_cols = chunk_heads * DH

    my_spans = lax.dynamic_slice_in_dim(span_order, my_index * tiles, tiles)
    window_span = my_spans[:, None] - reach + jnp.arange(window_spans, dtype=jnp.int32)[None, :]
    window_slot = jnp.sum(
        jnp.where(span_order[None, None, :] == window_span[:, :, None],
                  jnp.arange(slot_count, dtype=jnp.int32)[None, None, :], 0), axis=2)
    half = ctx_count // 2
    my_half = my_index // half
    my_q = my_index % half
    window_owner = window_slot // tiles
    owner_s = (my_q - window_owner % half) % half
    owner_k = (window_owner // half != my_half).astype(jnp.int32)
    window_row = window_slot % tiles
    index_table = jnp.concatenate([(owner_s * 2 + owner_k).reshape(-1), window_slot.reshape(-1), my_spans,
                                   jnp.stack([my_half, my_q]).astype(jnp.int32),
                                   window_row.reshape(-1)])
    query_start = doc_start.reshape(tiles, SPAN, 1)

    def cross_pairs():
        return [(i, i ^ half) for i in range(ctx_count)]

    def half_pairs(shift):
        return [(i, (i // half) * half + (i % half + shift) % half) for i in range(ctx_count)]

    attended = None
    query_grad = None
    key_grads = []
    value_grads = []
    for chunk in range(chunks):
        cols = slice(chunk * chunk_cols, (chunk + 1) * chunk_cols)
        pair = jnp.concatenate([key_rows[:, cols], value_rows[:, cols]], axis=1)
        partner = lax.ppermute(pair, "ctx", cross_pairs())
        pieces = []
        for shift in range(half):
            for data in (pair, partner):
                piece = data if shift == 0 else lax.ppermute(data, "ctx", half_pairs(shift))
                pieces.append(piece.reshape(tiles, SPAN, 2 * chunk_cols))
        head0 = chunk * chunk_heads
        aliased = chunk > 0
        head0 = chunk * chunk_heads
        in_specs = [
            pl.BlockSpec((tiles, SPAN, 1), lambda j, idx: (0, 0, 0)),
            pl.BlockSpec((local_rows, group_cols), lambda j, idx, h=head0: (0, h + j)),
            pl.BlockSpec((local_rows, group_cols), lambda j, idx, h=head0: (0, h + j)),
        ] + [pl.BlockSpec((tiles, SPAN, DH), lambda j, idx: (0, 0, j))] * (2 * half) + [
            pl.BlockSpec((tiles, SPAN, DH), lambda j, idx, n=chunk_heads: (0, 0, n + j))
        ] * (2 * half)
        operands = [index_table, query_start, queries, out_grad] + pieces + pieces
        aliases = {}
        if aliased:
            in_specs += [pl.BlockSpec(memory_space=pl.ANY), pl.BlockSpec(memory_space=pl.ANY)]
            operands += [attended, query_grad]
            aliases = {len(operands) - 2: 0, len(operands) - 1: 1}
        kernel = pl.pallas_call(
            lambda *refs, a=aliased: attention_kernel(
                *refs, group_size=group_size, window_spans=window_spans, tiles=tiles,
                half=half, score_scale=score_scale, aliased=a),
            grid_spec=pltpu.PrefetchScalarGridSpec(
                num_scalar_prefetch=1,
                grid=(chunk_heads,),
                in_specs=in_specs,
                out_specs=[
                    pl.BlockSpec((local_rows, group_cols), lambda j, idx, h=head0: (0, h + j)),
                    pl.BlockSpec((local_rows, group_cols), lambda j, idx, h=head0: (0, h + j)),
                ] + [pl.BlockSpec((2, 1, tiles, SPAN, 2 * DH), lambda j, idx: (0, j, 0, 0, 0))] * half,
                scratch_shapes=[pltpu.VMEM((slot_count, SPAN, 2 * DH), jnp.float32)],
            ),
            out_shape=[
                jax.ShapeDtypeStruct((local_rows, head_count * DH), jnp.bfloat16),
                jax.ShapeDtypeStruct((local_rows, head_count * DH), jnp.bfloat16),
                jax.ShapeDtypeStruct((2, chunk_heads, tiles, SPAN, 2 * DH), jnp.float32),
            ] + [jax.ShapeDtypeStruct((2, chunk_heads, tiles, SPAN, 2 * DH), jnp.bfloat16)] * (half - 1),
            input_output_aliases=aliases,
        )
        attended, query_grad, own_pack, *send_packs = kernel(*operands)

        pack_shape = (2, chunk_heads, local_rows, 2 * DH)
        summed = own_pack.reshape(pack_shape)
        for shift in range(1, half):
            summed = summed + lax.ppermute(
                send_packs[shift - 1].reshape(pack_shape), "ctx",
                half_pairs(shift)).astype(jnp.float32)
        summed = summed[0] + lax.ppermute(
            summed[1].astype(jnp.bfloat16), "ctx", cross_pairs()).astype(jnp.float32)
        key_grads.append(summed[:, :, :DH])
        value_grads.append(summed[:, :, DH:])

    def heads_to_cols(parts):
        stacked = jnp.concatenate(parts, axis=0)
        return stacked.transpose(1, 0, 2).reshape(local_rows, kv_count * DH).astype(jnp.bfloat16)

    return (attended, query_grad, heads_to_cols(key_grads), heads_to_cols(value_grads))


def solution(mesh):
    in_specs = (
        P(("groups", "ctx"), "head"),
        P(("groups", "ctx"), "head"),
        P(("groups", "ctx"), "head"),
        P(("groups", "ctx"), "head"),
        P(("groups", "ctx")),
        P("groups"),
    )
    out_specs = (
        P(("groups", "ctx"), "head"),
        P(("groups", "ctx"), "head"),
        P(("groups", "ctx"), "head"),
        P(("groups", "ctx"), "head"),
    )
    return jax.shard_map(local, mesh=mesh, in_specs=in_specs, out_specs=out_specs, check_vma=False)
```

```python
import math

import jax
import jax.numpy as jnp
from jax import lax
from jax.experimental import pallas as pl
from jax.experimental.pallas import tpu as pltpu
from jax.sharding import PartitionSpec as P

DH = 128
SPAN = 64
CHUNKS = 2


def attention_kernel(index_ref, qstart_ref, q_ref, do_ref,
                     *rest, group_size, window_spans, tiles, half, score_scale, aliased):
    key_refs = rest[:half]
    value_refs = rest[half:2 * half]
    rest = rest[2 * half:]
    if aliased:
        rest = rest[2:]
    out_ref, dq_ref, own_ref = rest[:3]
    send_refs = rest[3:-1]
    buf_ref = rest[-1]
    info = 2 * tiles * window_spans + tiles
    buf_ref[...] = jnp.zeros(buf_ref.shape, buf_ref.dtype)
    for tile in range(tiles):
        rows = slice(tile * SPAN, (tile + 1) * SPAN)
        base = tile * window_spans

        def window_rows(refs):
            parts = []
            for w in range(window_spans):
                piece = index_ref[base + w]
                row = index_ref[info + 2 + base + w]
                part = refs[0][row]
                for other in range(1, half):
                    part = jnp.where(piece == other, refs[other][row], part)
                parts.append(part)
            return jnp.concatenate(parts, axis=0)

        key_block = window_rows(key_refs)
        value_block = window_rows(value_refs)
        query_all = jnp.concatenate(
            [q_ref[rows, h * DH:(h + 1) * DH] for h in range(group_size)], axis=0)
        grad_all = jnp.concatenate(
            [do_ref[rows, h * DH:(h + 1) * DH] for h in range(group_size)], axis=0)
        span = index_ref[2 * tiles * window_spans + tile]
        window = window_spans * SPAN
        row_ids = lax.broadcasted_iota(jnp.int32, (SPAN, window), 0)
        col_ids = lax.broadcasted_iota(jnp.int32, (SPAN, window), 1)
        query_pos = span * SPAN + row_ids
        key_pos = (span - (window_spans - 1)) * SPAN + col_ids
        visible = (key_pos >= qstart_ref[tile]) & (key_pos <= query_pos)
        bias = jnp.where(visible, 0.0, -jnp.inf)
        bias = jnp.concatenate([bias] * group_size, axis=0)
        contract_last = (((1,), (1,)), ((), ()))
        contract_first = (((0,), (0,)), ((), ()))
        scores = lax.dot_general(query_all, key_block, contract_last,
                                 preferred_element_type=jnp.float32) * score_scale
        masked = scores + bias
        row_max = jnp.max(masked, axis=1, keepdims=True)
        shifted = jnp.exp(masked - row_max)
        log_totals = row_max + jnp.log(jnp.sum(shifted, axis=1, keepdims=True))
        weights = jnp.exp(masked - log_totals)
        weights_low = weights.astype(jnp.bfloat16)
        attended = jnp.dot(weights_low, value_block,
                           preferred_element_type=jnp.float32).astype(jnp.bfloat16)
        row_dots = jnp.sum(attended.astype(jnp.float32) * grad_all.astype(jnp.float32),
                           axis=1, keepdims=True)
        grad_weights = lax.dot_general(grad_all, value_block, contract_last,
                                       preferred_element_type=jnp.float32)
        grad_scores = (weights * (grad_weights - row_dots)).astype(jnp.bfloat16)
        query_grad = (jnp.dot(grad_scores, key_block, preferred_element_type=jnp.float32)
                      * score_scale).astype(jnp.bfloat16)
        for h in range(group_size):
            out_ref[rows, h * DH:(h + 1) * DH] = attended[h * SPAN:(h + 1) * SPAN]
            dq_ref[rows, h * DH:(h + 1) * DH] = query_grad[h * SPAN:(h + 1) * SPAN]
        key_sum = lax.dot_general(grad_scores, query_all, contract_first,
                                  preferred_element_type=jnp.float32) * score_scale
        value_sum = lax.dot_general(weights_low, grad_all, contract_first,
                                    preferred_element_type=jnp.float32)

        slot_base = tiles * window_spans + base
        for w in range(window_spans):
            slot = index_ref[slot_base + w]
            part = slice(w * SPAN, (w + 1) * SPAN)
            buf_ref[slot, :, :DH] += key_sum[part]
            buf_ref[slot, :, DH:] += value_sum[part]

    my_half = index_ref[info]
    my_q = index_ref[info + 1]
    for shift, ref in enumerate((own_ref,) + tuple(send_refs)):
        target = my_half * half + (my_q + shift) % half
        other = (target + half) % (2 * half)
        for k, device in enumerate((target, other)):
            block = buf_ref[pl.ds(device * tiles, tiles)]
            ref[k, 0] = block.astype(ref.dtype)


def local(queries, key_rows, value_rows, out_grad, doc_start, span_order):
    local_rows = queries.shape[0]
    tiles = local_rows // SPAN
    head_count = queries.shape[1] // DH
    kv_count = key_rows.shape[1] // DH
    group_size = head_count // kv_count
    group_cols = group_size * DH
    score_scale = 1.0 / math.sqrt(DH)
    ctx_count = lax.axis_size("ctx")
    my_index = lax.axis_index("ctx")
    total_rows = local_rows * ctx_count
    slot_count = total_rows // SPAN
    reach = total_rows // 4 // SPAN
    window_spans = reach + 1
    window = window_spans * SPAN
    chunks = CHUNKS if kv_count % CHUNKS == 0 else 1
    chunk_heads = kv_count // chunks
    chunk_cols = chunk_heads * DH

    my_spans = lax.dynamic_slice_in_dim(span_order, my_index * tiles, tiles)
    window_span = my_spans[:, None] - reach + jnp.arange(window_spans, dtype=jnp.int32)[None, :]
    window_slot = jnp.sum(
        jnp.where(span_order[None, None, :] == window_span[:, :, None],
                  jnp.arange(slot_count, dtype=jnp.int32)[None, None, :], 0), axis=2)
    half = ctx_count // 2
    my_half = my_index // half
    my_q = my_index % half
    window_owner = window_slot // tiles
    owner_s = (my_q - window_owner % half) % half
    owner_k = (window_owner // half != my_half).astype(jnp.int32)
    window_row = owner_k * tiles + window_slot % tiles
    index_table = jnp.concatenate([owner_s.reshape(-1), window_slot.reshape(-1), my_spans,
                                   jnp.stack([my_half, my_q]).astype(jnp.int32),
                                   window_row.reshape(-1)])
    query_start = doc_start.reshape(tiles, SPAN, 1)

    def cross_pairs():
        return [(i, i ^ half) for i in range(ctx_count)]

    def half_pairs(shift):
        return [(i, (i // half) * half + (i % half + shift) % half) for i in range(ctx_count)]

    attended = None
    query_grad = None
    key_grads = []
    value_grads = []
    pairs = [jnp.concatenate([key_rows[:, c * chunk_cols:(c + 1) * chunk_cols],
                              value_rows[:, c * chunk_cols:(c + 1) * chunk_cols]], axis=1)
             for c in range(chunks)]
    partners = []
    for chunk in range(chunks):
        partners.append(lax.ppermute(pairs[chunk], "ctx", cross_pairs()))
        if chunk + 1 < chunks:
            partners[chunk], pairs[chunk + 1] = lax.optimization_barrier(
                (partners[chunk], pairs[chunk + 1]))
    for chunk in range(chunks):
        pair = pairs[chunk]
        both = jnp.stack([pair, partners[chunk]])
        pieces = [both]
        for shift in range(1, half):
            pieces.append(lax.ppermute(both, "ctx", half_pairs(shift)))
        pieces = [piece.reshape(2 * tiles, SPAN, 2 * chunk_cols) for piece in pieces]

        aliased = chunk > 0
        head0 = chunk * chunk_heads
        in_specs = [
            pl.BlockSpec((tiles, SPAN, 1), lambda j, idx: (0, 0, 0)),
            pl.BlockSpec((local_rows, group_cols), lambda j, idx, h=head0: (0, h + j)),
            pl.BlockSpec((local_rows, group_cols), lambda j, idx, h=head0: (0, h + j)),
        ] + [pl.BlockSpec((2 * tiles, SPAN, DH), lambda j, idx: (0, 0, j))] * half + [
            pl.BlockSpec((2 * tiles, SPAN, DH), lambda j, idx, n=chunk_heads: (0, 0, n + j))
        ] * half
        operands = [index_table, query_start, queries, out_grad] + pieces + pieces
        aliases = {}
        if aliased:
            in_specs += [pl.BlockSpec(memory_space=pl.ANY), pl.BlockSpec(memory_space=pl.ANY)]
            operands += [attended, query_grad]
            aliases = {len(operands) - 2: 0, len(operands) - 1: 1}
        kernel = pl.pallas_call(
            lambda *refs, a=aliased: attention_kernel(
                *refs, group_size=group_size, window_spans=window_spans, tiles=tiles,
                half=half, score_scale=score_scale, aliased=a),
            grid_spec=pltpu.PrefetchScalarGridSpec(
                num_scalar_prefetch=1,
                grid=(chunk_heads,),
                in_specs=in_specs,
                out_specs=[
                    pl.BlockSpec((local_rows, group_cols), lambda j, idx, h=head0: (0, h + j)),
                    pl.BlockSpec((local_rows, group_cols), lambda j, idx, h=head0: (0, h + j)),
                ] + [pl.BlockSpec((2, 1, tiles, SPAN, 2 * DH), lambda j, idx: (0, j, 0, 0, 0))] * half,
                scratch_shapes=[pltpu.VMEM((slot_count, SPAN, 2 * DH), jnp.float32)],
            ),
            out_shape=[
                jax.ShapeDtypeStruct((local_rows, head_count * DH), jnp.bfloat16),
                jax.ShapeDtypeStruct((local_rows, head_count * DH), jnp.bfloat16),
                jax.ShapeDtypeStruct((2, chunk_heads, tiles, SPAN, 2 * DH), jnp.float32),
            ] + [jax.ShapeDtypeStruct((2, chunk_heads, tiles, SPAN, 2 * DH), jnp.bfloat16)] * (half - 1),
            input_output_aliases=aliases,
        )
        attended, query_grad, own_pack, *send_packs = kernel(*operands)

        pack_shape = (2, chunk_heads, local_rows, 2 * DH)
        summed = own_pack.reshape(pack_shape)
        for shift in range(1, half):
            summed = summed + lax.ppermute(
                send_packs[shift - 1].reshape(pack_shape), "ctx",
                half_pairs(shift)).astype(jnp.float32)
        summed = summed[0] + lax.ppermute(
            summed[1].astype(jnp.bfloat16), "ctx", cross_pairs()).astype(jnp.float32)
        key_grads.append(summed[:, :, :DH])
        value_grads.append(summed[:, :, DH:])

    def heads_to_cols(parts):
        stacked = jnp.concatenate(parts, axis=0)
        return stacked.transpose(1, 0, 2).reshape(local_rows, kv_count * DH).astype(jnp.bfloat16)

    return (attended, query_grad, heads_to_cols(key_grads), heads_to_cols(value_grads))


def solution(mesh):
    in_specs = (
        P(("groups", "ctx"), "head"),
        P(("groups", "ctx"), "head"),
        P(("groups", "ctx"), "head"),
        P(("groups", "ctx"), "head"),
        P(("groups", "ctx")),
        P("groups"),
    )
    out_specs = (
        P(("groups", "ctx"), "head"),
        P(("groups", "ctx"), "head"),
        P(("groups", "ctx"), "head"),
        P(("groups", "ctx"), "head"),
    )
    return jax.shard_map(local, mesh=mesh, in_specs=in_specs, out_specs=out_specs, check_vma=False)
```

```python
import math

import jax
import jax.numpy as jnp
from jax import lax
from jax.experimental import pallas as pl
from jax.experimental.pallas import tpu as pltpu
from jax.sharding import PartitionSpec as P

DH = 128
SPAN = 64
CHUNKS = 2


def attention_kernel(index_ref, qstart_ref, q_ref, do_ref,
                     *rest, group_size, window_spans, tiles, half, score_scale, aliased):
    key_refs = rest[:half]
    value_refs = rest[half:2 * half]
    rest = rest[2 * half:]
    if aliased:
        rest = rest[2:]
    out_ref, dq_ref, own_ref = rest[:3]
    send_refs = rest[3:-1]
    buf_ref = rest[-1]
    info = 2 * tiles * window_spans + tiles
    buf_ref[...] = jnp.zeros(buf_ref.shape, buf_ref.dtype)
    for tile in range(tiles):
        rows = slice(tile * SPAN, (tile + 1) * SPAN)
        base = tile * window_spans

        def window_rows(refs):
            parts = []
            for w in range(window_spans):
                piece = index_ref[base + w]
                row = index_ref[info + 2 + base + w]
                part = refs[0][row]
                for other in range(1, half):
                    part = jnp.where(piece == other, refs[other][row], part)
                parts.append(part)
            return jnp.concatenate(parts, axis=0)

        key_block = window_rows(key_refs)
        value_block = window_rows(value_refs)
        query_all = jnp.concatenate(
            [q_ref[rows, h * DH:(h + 1) * DH] for h in range(group_size)], axis=0)
        grad_all = jnp.concatenate(
            [do_ref[rows, h * DH:(h + 1) * DH] for h in range(group_size)], axis=0)
        span = index_ref[2 * tiles * window_spans + tile]
        window = window_spans * SPAN
        row_ids = lax.broadcasted_iota(jnp.int32, (SPAN, window), 0)
        col_ids = lax.broadcasted_iota(jnp.int32, (SPAN, window), 1)
        query_pos = span * SPAN + row_ids
        key_pos = (span - (window_spans - 1)) * SPAN + col_ids
        visible = (key_pos >= qstart_ref[tile]) & (key_pos <= query_pos)
        bias = jnp.where(visible, 0.0, -jnp.inf)
        bias = jnp.concatenate([bias] * group_size, axis=0)
        contract_last = (((1,), (1,)), ((), ()))
        contract_first = (((0,), (0,)), ((), ()))
        scores = lax.dot_general(query_all, key_block, contract_last,
                                 preferred_element_type=jnp.float32) * score_scale
        masked = scores + bias
        row_max = jnp.max(masked, axis=1, keepdims=True)
        shifted = jnp.exp(masked - row_max)
        log_totals = row_max + jnp.log(jnp.sum(shifted, axis=1, keepdims=True))
        weights = jnp.exp(masked - log_totals)
        weights_low = weights.astype(jnp.bfloat16)
        attended = jnp.dot(weights_low, value_block,
                           preferred_element_type=jnp.float32).astype(jnp.bfloat16)
        row_dots = jnp.sum(attended.astype(jnp.float32) * grad_all.astype(jnp.float32),
                           axis=1, keepdims=True)
        grad_weights = lax.dot_general(grad_all, value_block, contract_last,
                                       preferred_element_type=jnp.float32)
        grad_scores = (weights * (grad_weights - row_dots)).astype(jnp.bfloat16)
        query_grad = (jnp.dot(grad_scores, key_block, preferred_element_type=jnp.float32)
                      * score_scale).astype(jnp.bfloat16)
        for h in range(group_size):
            out_ref[rows, h * DH:(h + 1) * DH] = attended[h * SPAN:(h + 1) * SPAN]
            dq_ref[rows, h * DH:(h + 1) * DH] = query_grad[h * SPAN:(h + 1) * SPAN]
        key_sum = lax.dot_general(grad_scores, query_all, contract_first,
                                  preferred_element_type=jnp.float32) * score_scale
        value_sum = lax.dot_general(weights_low, grad_all, contract_first,
                                    preferred_element_type=jnp.float32)

        slot_base = tiles * window_spans + base
        for w in range(window_spans):
            slot = index_ref[slot_base + w]
            part = slice(w * SPAN, (w + 1) * SPAN)
            buf_ref[slot, :, :DH] += key_sum[part]
            buf_ref[slot, :, DH:] += value_sum[part]

    my_half = index_ref[info]
    my_q = index_ref[info + 1]
    for shift, ref in enumerate((own_ref,) + tuple(send_refs)):
        target = my_half * half + (my_q + shift) % half
        other = (target + half) % (2 * half)
        for k, device in enumerate((target, other)):
            block = buf_ref[pl.ds(device * tiles, tiles)]
            ref[k, 0] = block.astype(ref.dtype)


def local(queries, key_rows, value_rows, out_grad, doc_start, span_order):
    local_rows = queries.shape[0]
    tiles = local_rows // SPAN
    head_count = queries.shape[1] // DH
    kv_count = key_rows.shape[1] // DH
    group_size = head_count // kv_count
    group_cols = group_size * DH
    score_scale = 1.0 / math.sqrt(DH)
    ctx_count = lax.axis_size("ctx")
    my_index = lax.axis_index("ctx")
    total_rows = local_rows * ctx_count
    slot_count = total_rows // SPAN
    reach = total_rows // 4 // SPAN
    window_spans = reach + 1
    window = window_spans * SPAN
    chunks = CHUNKS if kv_count % CHUNKS == 0 else 1
    chunk_heads = kv_count // chunks
    chunk_cols = chunk_heads * DH

    my_spans = lax.dynamic_slice_in_dim(span_order, my_index * tiles, tiles)
    window_span = my_spans[:, None] - reach + jnp.arange(window_spans, dtype=jnp.int32)[None, :]
    window_slot = jnp.sum(
        jnp.where(span_order[None, None, :] == window_span[:, :, None],
                  jnp.arange(slot_count, dtype=jnp.int32)[None, None, :], 0), axis=2)
    half = ctx_count // 2
    my_half = my_index // half
    my_q = my_index % half
    window_owner = window_slot // tiles
    owner_s = (my_q - window_owner % half) % half
    owner_k = (window_owner // half != my_half).astype(jnp.int32)
    window_row = owner_k * tiles + window_slot % tiles
    index_table = jnp.concatenate([owner_s.reshape(-1), window_slot.reshape(-1), my_spans,
                                   jnp.stack([my_half, my_q]).astype(jnp.int32),
                                   window_row.reshape(-1)])
    query_start = doc_start.reshape(tiles, SPAN, 1)

    def cross_pairs():
        return [(i, i ^ half) for i in range(ctx_count)]

    def half_pairs(shift):
        return [(i, (i // half) * half + (i % half + shift) % half) for i in range(ctx_count)]

    attended = None
    query_grad = None
    key_grads = []
    value_grads = []
    partner_keys = lax.ppermute(key_rows, "ctx", cross_pairs())
    partner_values = lax.ppermute(value_rows, "ctx", cross_pairs())
    for chunk in range(chunks):
        cols = slice(chunk * chunk_cols, (chunk + 1) * chunk_cols)
        pair = jnp.concatenate([key_rows[:, cols], value_rows[:, cols]], axis=1)
        partner = jnp.concatenate([partner_keys[:, cols], partner_values[:, cols]], axis=1)
        both = jnp.stack([pair, partner])
        pieces = [both]
        for shift in range(1, half):
            pieces.append(lax.ppermute(both, "ctx", half_pairs(shift)))
        pieces = [piece.reshape(2 * tiles, SPAN, 2 * chunk_cols) for piece in pieces]

        aliased = chunk > 0
        head0 = chunk * chunk_heads
        in_specs = [
            pl.BlockSpec((tiles, SPAN, 1), lambda j, idx: (0, 0, 0)),
            pl.BlockSpec((local_rows, group_cols), lambda j, idx, h=head0: (0, h + j)),
            pl.BlockSpec((local_rows, group_cols), lambda j, idx, h=head0: (0, h + j)),
        ] + [pl.BlockSpec((2 * tiles, SPAN, DH), lambda j, idx: (0, 0, j))] * half + [
            pl.BlockSpec((2 * tiles, SPAN, DH), lambda j, idx, n=chunk_heads: (0, 0, n + j))
        ] * half
        operands = [index_table, query_start, queries, out_grad] + pieces + pieces
        aliases = {}
        if aliased:
            in_specs += [pl.BlockSpec(memory_space=pl.ANY), pl.BlockSpec(memory_space=pl.ANY)]
            operands += [attended, query_grad]
            aliases = {len(operands) - 2: 0, len(operands) - 1: 1}
        kernel = pl.pallas_call(
            lambda *refs, a=aliased: attention_kernel(
                *refs, group_size=group_size, window_spans=window_spans, tiles=tiles,
                half=half, score_scale=score_scale, aliased=a),
            grid_spec=pltpu.PrefetchScalarGridSpec(
                num_scalar_prefetch=1,
                grid=(chunk_heads,),
                in_specs=in_specs,
                out_specs=[
                    pl.BlockSpec((local_rows, group_cols), lambda j, idx, h=head0: (0, h + j)),
                    pl.BlockSpec((local_rows, group_cols), lambda j, idx, h=head0: (0, h + j)),
                ] + [pl.BlockSpec((2, 1, tiles, SPAN, 2 * DH), lambda j, idx: (0, j, 0, 0, 0))] * half,
                scratch_shapes=[pltpu.VMEM((slot_count, SPAN, 2 * DH), jnp.float32)],
            ),
            out_shape=[
                jax.ShapeDtypeStruct((local_rows, head_count * DH), jnp.bfloat16),
                jax.ShapeDtypeStruct((local_rows, head_count * DH), jnp.bfloat16),
                jax.ShapeDtypeStruct((2, chunk_heads, tiles, SPAN, 2 * DH), jnp.float32),
            ] + [jax.ShapeDtypeStruct((2, chunk_heads, tiles, SPAN, 2 * DH), jnp.bfloat16)] * (half - 1),
            input_output_aliases=aliases,
        )
        attended, query_grad, own_pack, *send_packs = kernel(*operands)

        pack_shape = (2, chunk_heads, local_rows, 2 * DH)
        summed = own_pack.reshape(pack_shape)
        for shift in range(1, half):
            summed = summed + lax.ppermute(
                send_packs[shift - 1].reshape(pack_shape), "ctx",
                half_pairs(shift)).astype(jnp.float32)
        summed = summed[0] + lax.ppermute(
            summed[1].astype(jnp.bfloat16), "ctx", cross_pairs()).astype(jnp.float32)
        key_grads.append(summed[:, :, :DH])
        value_grads.append(summed[:, :, DH:])

    def heads_to_cols(parts):
        stacked = jnp.concatenate(parts, axis=0)
        return stacked.transpose(1, 0, 2).reshape(local_rows, kv_count * DH).astype(jnp.bfloat16)

    return (attended, query_grad, heads_to_cols(key_grads), heads_to_cols(value_grads))


def solution(mesh):
    in_specs = (
        P(("groups", "ctx"), "head"),
        P(("groups", "ctx"), "head"),
        P(("groups", "ctx"), "head"),
        P(("groups", "ctx"), "head"),
        P(("groups", "ctx")),
        P("groups"),
    )
    out_specs = (
        P(("groups", "ctx"), "head"),
        P(("groups", "ctx"), "head"),
        P(("groups", "ctx"), "head"),
        P(("groups", "ctx"), "head"),
    )
    return jax.shard_map(local, mesh=mesh, in_specs=in_specs, out_specs=out_specs, check_vma=False)
```

```python
import math

import jax
import jax.numpy as jnp
from jax import lax
from jax.experimental import pallas as pl
from jax.experimental.pallas import tpu as pltpu
from jax.sharding import PartitionSpec as P

DH = 128
SPAN = 64
CHUNKS = 2


def attention_kernel(index_ref, qstart_ref, q_ref, do_ref,
                     *rest, group_size, window_spans, tiles, half, score_scale, aliased):
    key_refs = rest[:half]
    value_refs = rest[half:2 * half]
    rest = rest[2 * half:]
    if aliased:
        rest = rest[2:]
    out_ref, dq_ref, own_ref = rest[:3]
    send_refs = rest[3:-1]
    buf_ref = rest[-1]
    info = 2 * tiles * window_spans + tiles
    buf_ref[...] = jnp.zeros(buf_ref.shape, buf_ref.dtype)
    for tile in range(tiles):
        rows = slice(tile * SPAN, (tile + 1) * SPAN)
        base = tile * window_spans

        def window_rows(refs):
            parts = []
            for w in range(window_spans):
                piece = index_ref[base + w]
                row = index_ref[info + 2 + base + w]
                part = refs[0][row]
                for other in range(1, half):
                    part = jnp.where(piece == other, refs[other][row], part)
                parts.append(part)
            return jnp.concatenate(parts, axis=0)

        key_block = window_rows(key_refs)
        value_block = window_rows(value_refs)
        query_all = jnp.concatenate(
            [q_ref[rows, h * DH:(h + 1) * DH] for h in range(group_size)], axis=0)
        grad_all = jnp.concatenate(
            [do_ref[rows, h * DH:(h + 1) * DH] for h in range(group_size)], axis=0)
        span = index_ref[2 * tiles * window_spans + tile]
        window = window_spans * SPAN
        row_ids = lax.broadcasted_iota(jnp.int32, (SPAN, window), 0)
        col_ids = lax.broadcasted_iota(jnp.int32, (SPAN, window), 1)
        query_pos = span * SPAN + row_ids
        key_pos = (span - (window_spans - 1)) * SPAN + col_ids
        visible = (key_pos >= qstart_ref[tile]) & (key_pos <= query_pos)
        bias = jnp.where(visible, 0.0, -jnp.inf)
        bias = jnp.concatenate([bias] * group_size, axis=0)
        contract_last = (((1,), (1,)), ((), ()))
        contract_first = (((0,), (0,)), ((), ()))
        scores = lax.dot_general(query_all, key_block, contract_last,
                                 preferred_element_type=jnp.float32) * score_scale
        masked = scores + bias
        row_max = jnp.max(masked, axis=1, keepdims=True)
        shifted = jnp.exp(masked - row_max)
        weights = shifted * (1.0 / jnp.sum(shifted, axis=1, keepdims=True))
        weights_low = weights.astype(jnp.bfloat16)
        attended = jnp.dot(weights_low, value_block,
                           preferred_element_type=jnp.float32).astype(jnp.bfloat16)
        row_dots = jnp.sum(attended.astype(jnp.float32) * grad_all.astype(jnp.float32),
                           axis=1, keepdims=True)
        grad_weights = lax.dot_general(grad_all, value_block, contract_last,
                                       preferred_element_type=jnp.float32)
        grad_scores = (weights * (grad_weights - row_dots)).astype(jnp.bfloat16)
        query_grad = (jnp.dot(grad_scores, key_block, preferred_element_type=jnp.float32)
                      * score_scale).astype(jnp.bfloat16)
        for h in range(group_size):
            out_ref[rows, h * DH:(h + 1) * DH] = attended[h * SPAN:(h + 1) * SPAN]
            dq_ref[rows, h * DH:(h + 1) * DH] = query_grad[h * SPAN:(h + 1) * SPAN]
        key_sum = lax.dot_general(grad_scores, query_all, contract_first,
                                  preferred_element_type=jnp.float32) * score_scale
        value_sum = lax.dot_general(weights_low, grad_all, contract_first,
                                    preferred_element_type=jnp.float32)

        slot_base = tiles * window_spans + base
        for w in range(window_spans):
            slot = index_ref[slot_base + w]
            part = slice(w * SPAN, (w + 1) * SPAN)
            buf_ref[slot, :, :DH] += key_sum[part]
            buf_ref[slot, :, DH:] += value_sum[part]

    my_half = index_ref[info]
    my_q = index_ref[info + 1]
    for shift, ref in enumerate((own_ref,) + tuple(send_refs)):
        target = my_half * half + (my_q + shift) % half
        other = (target + half) % (2 * half)
        for k, device in enumerate((target, other)):
            block = buf_ref[pl.ds(device * tiles, tiles)]
            ref[k, 0] = block.astype(ref.dtype)


def local(queries, key_rows, value_rows, out_grad, doc_start, span_order):
    local_rows = queries.shape[0]
    tiles = local_rows // SPAN
    head_count = queries.shape[1] // DH
    kv_count = key_rows.shape[1] // DH
    group_size = head_count // kv_count
    group_cols = group_size * DH
    score_scale = 1.0 / math.sqrt(DH)
    ctx_count = lax.axis_size("ctx")
    my_index = lax.axis_index("ctx")
    total_rows = local_rows * ctx_count
    slot_count = total_rows // SPAN
    reach = total_rows // 4 // SPAN
    window_spans = reach + 1
    window = window_spans * SPAN
    chunks = CHUNKS if kv_count % CHUNKS == 0 else 1
    chunk_heads = kv_count // chunks
    chunk_cols = chunk_heads * DH

    my_spans = lax.dynamic_slice_in_dim(span_order, my_index * tiles, tiles)
    window_span = my_spans[:, None] - reach + jnp.arange(window_spans, dtype=jnp.int32)[None, :]
    window_slot = jnp.sum(
        jnp.where(span_order[None, None, :] == window_span[:, :, None],
                  jnp.arange(slot_count, dtype=jnp.int32)[None, None, :], 0), axis=2)
    half = ctx_count // 2
    my_half = my_index // half
    my_q = my_index % half
    window_owner = window_slot // tiles
    owner_s = (my_q - window_owner % half) % half
    owner_k = (window_owner // half != my_half).astype(jnp.int32)
    window_row = owner_k * tiles + window_slot % tiles
    index_table = jnp.concatenate([owner_s.reshape(-1), window_slot.reshape(-1), my_spans,
                                   jnp.stack([my_half, my_q]).astype(jnp.int32),
                                   window_row.reshape(-1)])
    query_start = doc_start.reshape(tiles, SPAN, 1)

    def cross_pairs():
        return [(i, i ^ half) for i in range(ctx_count)]

    def half_pairs(shift):
        return [(i, (i // half) * half + (i % half + shift) % half) for i in range(ctx_count)]

    attended = None
    query_grad = None
    key_grads = []
    value_grads = []
    for chunk in range(chunks):
        cols = slice(chunk * chunk_cols, (chunk + 1) * chunk_cols)
        pair = jnp.concatenate([key_rows[:, cols], value_rows[:, cols]], axis=1)
        both = jnp.stack([pair, lax.ppermute(pair, "ctx", cross_pairs())])
        pieces = [both]
        for shift in range(1, half):
            pieces.append(lax.ppermute(both, "ctx", half_pairs(shift)))
        pieces = [piece.reshape(2 * tiles, SPAN, 2 * chunk_cols) for piece in pieces]

        aliased = chunk > 0
        head0 = chunk * chunk_heads
        in_specs = [
            pl.BlockSpec((tiles, SPAN, 1), lambda j, idx: (0, 0, 0)),
            pl.BlockSpec((local_rows, group_cols), lambda j, idx, h=head0: (0, h + j)),
            pl.BlockSpec((local_rows, group_cols), lambda j, idx, h=head0: (0, h + j)),
        ] + [pl.BlockSpec((2 * tiles, SPAN, DH), lambda j, idx: (0, 0, j))] * half + [
            pl.BlockSpec((2 * tiles, SPAN, DH), lambda j, idx, n=chunk_heads: (0, 0, n + j))
        ] * half
        operands = [index_table, query_start, queries, out_grad] + pieces + pieces
        aliases = {}
        if aliased:
            in_specs += [pl.BlockSpec(memory_space=pl.ANY), pl.BlockSpec(memory_space=pl.ANY)]
            operands += [attended, query_grad]
            aliases = {len(operands) - 2: 0, len(operands) - 1: 1}
        kernel = pl.pallas_call(
            lambda *refs, a=aliased: attention_kernel(
                *refs, group_size=group_size, window_spans=window_spans, tiles=tiles,
                half=half, score_scale=score_scale, aliased=a),
            grid_spec=pltpu.PrefetchScalarGridSpec(
                num_scalar_prefetch=1,
                grid=(chunk_heads,),
                in_specs=in_specs,
                out_specs=[
                    pl.BlockSpec((local_rows, group_cols), lambda j, idx, h=head0: (0, h + j)),
                    pl.BlockSpec((local_rows, group_cols), lambda j, idx, h=head0: (0, h + j)),
                ] + [pl.BlockSpec((2, 1, tiles, SPAN, 2 * DH), lambda j, idx: (0, j, 0, 0, 0))] * half,
                scratch_shapes=[pltpu.VMEM((slot_count, SPAN, 2 * DH), jnp.float32)],
            ),
            out_shape=[
                jax.ShapeDtypeStruct((local_rows, head_count * DH), jnp.bfloat16),
                jax.ShapeDtypeStruct((local_rows, head_count * DH), jnp.bfloat16),
                jax.ShapeDtypeStruct((2, chunk_heads, tiles, SPAN, 2 * DH), jnp.float32),
            ] + [jax.ShapeDtypeStruct((2, chunk_heads, tiles, SPAN, 2 * DH), jnp.bfloat16)] * (half - 1),
            input_output_aliases=aliases,
        )
        attended, query_grad, own_pack, *send_packs = kernel(*operands)

        pack_shape = (2, chunk_heads, local_rows, 2 * DH)
        summed = own_pack.reshape(pack_shape)
        for shift in range(1, half):
            summed = summed + lax.ppermute(
                send_packs[shift - 1].reshape(pack_shape), "ctx",
                half_pairs(shift)).astype(jnp.float32)
        summed = summed[0] + lax.ppermute(
            summed[1].astype(jnp.bfloat16), "ctx", cross_pairs()).astype(jnp.float32)
        key_grads.append(summed[:, :, :DH])
        value_grads.append(summed[:, :, DH:])

    def heads_to_cols(parts):
        stacked = jnp.concatenate(parts, axis=0)
        return stacked.transpose(1, 0, 2).reshape(local_rows, kv_count * DH).astype(jnp.bfloat16)

    return (attended, query_grad, heads_to_cols(key_grads), heads_to_cols(value_grads))


def solution(mesh):
    in_specs = (
        P(("groups", "ctx"), "head"),
        P(("groups", "ctx"), "head"),
        P(("groups", "ctx"), "head"),
        P(("groups", "ctx"), "head"),
        P(("groups", "ctx")),
        P("groups"),
    )
    out_specs = (
        P(("groups", "ctx"), "head"),
        P(("groups", "ctx"), "head"),
        P(("groups", "ctx"), "head"),
        P(("groups", "ctx"), "head"),
    )
    return jax.shard_map(local, mesh=mesh, in_specs=in_specs, out_specs=out_specs, check_vma=False)
```

```python
import math

import jax
import jax.numpy as jnp
from jax import lax
from jax.experimental import pallas as pl
from jax.experimental.pallas import tpu as pltpu
from jax.sharding import PartitionSpec as P

DH = 128
SPAN = 64
CHUNKS = 2


def attention_kernel(index_ref, qstart_ref, q_ref, do_ref,
                     *rest, group_size, window_spans, tiles, half, score_scale, aliased):
    key_refs = rest[:half]
    value_refs = rest[half:2 * half]
    rest = rest[2 * half:]
    if aliased:
        rest = rest[2:]
    out_ref, dq_ref, own_ref = rest[:3]
    send_refs = rest[3:-1]
    buf_ref = rest[-1]
    info = 2 * tiles * window_spans + tiles
    buf_ref[...] = jnp.zeros(buf_ref.shape, buf_ref.dtype)
    for tile in range(tiles):
        rows = slice(tile * SPAN, (tile + 1) * SPAN)
        base = tile * window_spans

        def window_rows(refs):
            parts = []
            for w in range(window_spans):
                piece = index_ref[base + w]
                row = index_ref[info + 2 + base + w]
                part = refs[0][row]
                for other in range(1, half):
                    part = jnp.where(piece == other, refs[other][row], part)
                parts.append(part)
            return jnp.concatenate(parts, axis=0)

        key_block = window_rows(key_refs)
        value_block = window_rows(value_refs)
        query_all = jnp.concatenate(
            [q_ref[rows, h * DH:(h + 1) * DH] for h in range(group_size)], axis=0)
        grad_all = jnp.concatenate(
            [do_ref[rows, h * DH:(h + 1) * DH] for h in range(group_size)], axis=0)
        span = index_ref[2 * tiles * window_spans + tile]
        window = window_spans * SPAN
        row_ids = lax.broadcasted_iota(jnp.int32, (SPAN, window), 0)
        col_ids = lax.broadcasted_iota(jnp.int32, (SPAN, window), 1)
        query_pos = span * SPAN + row_ids
        key_pos = (span - (window_spans - 1)) * SPAN + col_ids
        visible = (key_pos >= qstart_ref[tile]) & (key_pos <= query_pos)
        bias = jnp.where(visible, 0.0, -jnp.inf)
        bias = jnp.concatenate([bias] * group_size, axis=0)
        contract_last = (((1,), (1,)), ((), ()))
        contract_first = (((0,), (0,)), ((), ()))
        scores = lax.dot_general(query_all, key_block, contract_last,
                                 preferred_element_type=jnp.float32) * score_scale
        masked = scores + bias
        row_max = jnp.max(masked, axis=1, keepdims=True)
        shifted = jnp.exp(masked - row_max)
        weights = shifted * (1.0 / jnp.sum(shifted, axis=1, keepdims=True))
        weights_low = weights.astype(jnp.bfloat16)
        attended = jnp.dot(weights_low, value_block,
                           preferred_element_type=jnp.float32).astype(jnp.bfloat16)
        row_dots = jnp.sum(attended.astype(jnp.float32) * grad_all.astype(jnp.float32),
                           axis=1, keepdims=True)
        grad_weights = lax.dot_general(grad_all, value_block, contract_last,
                                       preferred_element_type=jnp.float32)
        grad_scores = (weights * (grad_weights - row_dots)).astype(jnp.bfloat16)
        query_grad = (jnp.dot(grad_scores, key_block, preferred_element_type=jnp.float32)
                      * score_scale).astype(jnp.bfloat16)
        for h in range(group_size):
            out_ref[rows, h * DH:(h + 1) * DH] = attended[h * SPAN:(h + 1) * SPAN]
            dq_ref[rows, h * DH:(h + 1) * DH] = query_grad[h * SPAN:(h + 1) * SPAN]
        key_sum = lax.dot_general(grad_scores, query_all, contract_first,
                                  preferred_element_type=jnp.float32) * score_scale
        value_sum = lax.dot_general(weights_low, grad_all, contract_first,
                                    preferred_element_type=jnp.float32)

        slot_base = tiles * window_spans + base
        for w in range(window_spans):
            slot = index_ref[slot_base + w]
            part = slice(w * SPAN, (w + 1) * SPAN)
            buf_ref[slot, :, :DH] += key_sum[part]
            buf_ref[slot, :, DH:] += value_sum[part]

    my_half = index_ref[info]
    my_q = index_ref[info + 1]
    for shift, ref in enumerate((own_ref,) + tuple(send_refs)):
        target = my_half * half + (my_q + shift) % half
        other = (target + half) % (2 * half)
        for k, device in enumerate((target, other)):
            block = buf_ref[pl.ds(device * tiles, tiles)]
            ref[k, 0] = block.astype(ref.dtype)


def local(queries, key_rows, value_rows, out_grad, doc_start, span_order):
    local_rows = queries.shape[0]
    tiles = local_rows // SPAN
    head_count = queries.shape[1] // DH
    kv_count = key_rows.shape[1] // DH
    group_size = head_count // kv_count
    group_cols = group_size * DH
    score_scale = 1.0 / math.sqrt(DH)
    ctx_count = lax.axis_size("ctx")
    my_index = lax.axis_index("ctx")
    total_rows = local_rows * ctx_count
    slot_count = total_rows // SPAN
    reach = total_rows // 4 // SPAN
    window_spans = reach + 1
    window = window_spans * SPAN
    chunks = CHUNKS if kv_count % CHUNKS == 0 else 1
    chunk_heads = kv_count // chunks
    chunk_cols = chunk_heads * DH

    my_spans = lax.dynamic_slice_in_dim(span_order, my_index * tiles, tiles)
    window_span = my_spans[:, None] - reach + jnp.arange(window_spans, dtype=jnp.int32)[None, :]
    window_slot = jnp.sum(
        jnp.where(span_order[None, None, :] == window_span[:, :, None],
                  jnp.arange(slot_count, dtype=jnp.int32)[None, None, :], 0), axis=2)
    half = ctx_count // 2
    my_half = my_index // half
    my_q = my_index % half
    window_owner = window_slot // tiles
    owner_s = (my_q - window_owner % half) % half
    owner_k = (window_owner // half != my_half).astype(jnp.int32)
    window_row = owner_k * tiles + window_slot % tiles
    index_table = jnp.concatenate([owner_s.reshape(-1), window_slot.reshape(-1), my_spans,
                                   jnp.stack([my_half, my_q]).astype(jnp.int32),
                                   window_row.reshape(-1)])
    query_start = doc_start.reshape(tiles, SPAN, 1)

    def cross_pairs():
        return [(i, i ^ half) for i in range(ctx_count)]

    def half_pairs(shift):
        return [(i, (i // half) * half + (i % half + shift) % half) for i in range(ctx_count)]

    attended = None
    query_grad = None
    key_grads = []
    value_grads = []
    for chunk in range(chunks):
        cols = slice(chunk * chunk_cols, (chunk + 1) * chunk_cols)
        pair = jnp.concatenate([key_rows[:, cols], value_rows[:, cols]], axis=1)
        if chunk == 0:
            both = jnp.stack([pair, lax.ppermute(pair, "ctx", cross_pairs())])
            pieces = [both]
            for shift in range(1, half):
                pieces.append(lax.ppermute(both, "ctx", half_pairs(shift)))
        else:
            around = [pair] + [lax.ppermute(pair, "ctx", half_pairs(shift))
                               for shift in range(1, half)]
            crossed = lax.ppermute(jnp.stack(around), "ctx", cross_pairs())
            pieces = [jnp.stack([around[shift], crossed[shift]]) for shift in range(half)]
        pieces = [piece.reshape(2 * tiles, SPAN, 2 * chunk_cols) for piece in pieces]

        aliased = chunk > 0
        head0 = chunk * chunk_heads
        in_specs = [
            pl.BlockSpec((tiles, SPAN, 1), lambda j, idx: (0, 0, 0)),
            pl.BlockSpec((local_rows, group_cols), lambda j, idx, h=head0: (0, h + j)),
            pl.BlockSpec((local_rows, group_cols), lambda j, idx, h=head0: (0, h + j)),
        ] + [pl.BlockSpec((2 * tiles, SPAN, DH), lambda j, idx: (0, 0, j))] * half + [
            pl.BlockSpec((2 * tiles, SPAN, DH), lambda j, idx, n=chunk_heads: (0, 0, n + j))
        ] * half
        operands = [index_table, query_start, queries, out_grad] + pieces + pieces
        aliases = {}
        if aliased:
            in_specs += [pl.BlockSpec(memory_space=pl.ANY), pl.BlockSpec(memory_space=pl.ANY)]
            operands += [attended, query_grad]
            aliases = {len(operands) - 2: 0, len(operands) - 1: 1}
        kernel = pl.pallas_call(
            lambda *refs, a=aliased: attention_kernel(
                *refs, group_size=group_size, window_spans=window_spans, tiles=tiles,
                half=half, score_scale=score_scale, aliased=a),
            grid_spec=pltpu.PrefetchScalarGridSpec(
                num_scalar_prefetch=1,
                grid=(chunk_heads,),
                in_specs=in_specs,
                out_specs=[
                    pl.BlockSpec((local_rows, group_cols), lambda j, idx, h=head0: (0, h + j)),
                    pl.BlockSpec((local_rows, group_cols), lambda j, idx, h=head0: (0, h + j)),
                ] + [pl.BlockSpec((2, 1, tiles, SPAN, 2 * DH), lambda j, idx: (0, j, 0, 0, 0))] * half,
                scratch_shapes=[pltpu.VMEM((slot_count, SPAN, 2 * DH), jnp.float32)],
            ),
            out_shape=[
                jax.ShapeDtypeStruct((local_rows, head_count * DH), jnp.bfloat16),
                jax.ShapeDtypeStruct((local_rows, head_count * DH), jnp.bfloat16),
                jax.ShapeDtypeStruct((2, chunk_heads, tiles, SPAN, 2 * DH), jnp.float32),
            ] + [jax.ShapeDtypeStruct((2, chunk_heads, tiles, SPAN, 2 * DH), jnp.bfloat16)] * (half - 1),
            input_output_aliases=aliases,
        )
        attended, query_grad, own_pack, *send_packs = kernel(*operands)

        pack_shape = (2, chunk_heads, local_rows, 2 * DH)
        summed = own_pack.reshape(pack_shape)
        for shift in range(1, half):
            summed = summed + lax.ppermute(
                send_packs[shift - 1].reshape(pack_shape), "ctx",
                half_pairs(shift)).astype(jnp.float32)
        summed = summed[0] + lax.ppermute(
            summed[1].astype(jnp.bfloat16), "ctx", cross_pairs()).astype(jnp.float32)
        key_grads.append(summed[:, :, :DH])
        value_grads.append(summed[:, :, DH:])

    def heads_to_cols(parts):
        stacked = jnp.concatenate(parts, axis=0)
        return stacked.transpose(1, 0, 2).reshape(local_rows, kv_count * DH).astype(jnp.bfloat16)

    return (attended, query_grad, heads_to_cols(key_grads), heads_to_cols(value_grads))


def solution(mesh):
    in_specs = (
        P(("groups", "ctx"), "head"),
        P(("groups", "ctx"), "head"),
        P(("groups", "ctx"), "head"),
        P(("groups", "ctx"), "head"),
        P(("groups", "ctx")),
        P("groups"),
    )
    out_specs = (
        P(("groups", "ctx"), "head"),
        P(("groups", "ctx"), "head"),
        P(("groups", "ctx"), "head"),
        P(("groups", "ctx"), "head"),
    )
    return jax.shard_map(local, mesh=mesh, in_specs=in_specs, out_specs=out_specs, check_vma=False)
```

```python
import math

import jax
import jax.numpy as jnp
from jax import lax
from jax.experimental import pallas as pl
from jax.experimental.pallas import tpu as pltpu
from jax.sharding import PartitionSpec as P

DH = 128
SPAN = 64
CHUNKS = 2


def attention_kernel(index_ref, qstart_ref, q_ref, do_ref,
                     *rest, group_size, window_spans, tiles, half, score_scale, aliased):
    key_refs = rest[:half]
    value_refs = rest[half:2 * half]
    rest = rest[2 * half:]
    if aliased:
        rest = rest[2:]
    out_ref, dq_ref, own_ref = rest[:3]
    send_refs = rest[3:-1]
    buf_ref = rest[-1]
    info = 2 * tiles * window_spans + tiles
    buf_ref[...] = jnp.zeros(buf_ref.shape, buf_ref.dtype)
    for tile in range(tiles):
        rows = slice(tile * SPAN, (tile + 1) * SPAN)
        base = tile * window_spans

        def window_rows(refs):
            parts = []
            for w in range(window_spans):
                piece = index_ref[base + w]
                row = index_ref[info + 2 + base + w]
                part = refs[0][row]
                for other in range(1, half):
                    part = jnp.where(piece == other, refs[other][row], part)
                parts.append(part)
            return jnp.concatenate(parts, axis=0)

        key_block = window_rows(key_refs)
        value_block = window_rows(value_refs)
        query_all = jnp.concatenate(
            [q_ref[rows, h * DH:(h + 1) * DH] for h in range(group_size)], axis=0)
        grad_all = jnp.concatenate(
            [do_ref[rows, h * DH:(h + 1) * DH] for h in range(group_size)], axis=0)
        span = index_ref[2 * tiles * window_spans + tile]
        window = window_spans * SPAN
        row_ids = lax.broadcasted_iota(jnp.int32, (SPAN, window), 0)
        col_ids = lax.broadcasted_iota(jnp.int32, (SPAN, window), 1)
        query_pos = span * SPAN + row_ids
        key_pos = (span - (window_spans - 1)) * SPAN + col_ids
        visible = (key_pos >= qstart_ref[tile]) & (key_pos <= query_pos)
        bias = jnp.where(visible, 0.0, -jnp.inf)
        bias = jnp.concatenate([bias] * group_size, axis=0)
        contract_last = (((1,), (1,)), ((), ()))
        contract_first = (((0,), (0,)), ((), ()))
        scores = lax.dot_general(query_all, key_block, contract_last,
                                 preferred_element_type=jnp.float32) * score_scale
        masked = scores + bias
        row_max = jnp.max(masked, axis=1, keepdims=True)
        shifted = jnp.exp(masked - row_max)
        weights = shifted * (1.0 / jnp.sum(shifted, axis=1, keepdims=True))
        weights_low = weights.astype(jnp.bfloat16)
        attended = jnp.dot(weights_low, value_block,
                           preferred_element_type=jnp.float32).astype(jnp.bfloat16)
        row_dots = jnp.sum(attended.astype(jnp.float32) * grad_all.astype(jnp.float32),
                           axis=1, keepdims=True)
        grad_weights = lax.dot_general(grad_all, value_block, contract_last,
                                       preferred_element_type=jnp.float32)
        grad_scores = (weights * (grad_weights - row_dots)).astype(jnp.bfloat16)
        query_grad = (jnp.dot(grad_scores, key_block, preferred_element_type=jnp.float32)
                      * score_scale).astype(jnp.bfloat16)
        for h in range(group_size):
            out_ref[rows, h * DH:(h + 1) * DH] = attended[h * SPAN:(h + 1) * SPAN]
            dq_ref[rows, h * DH:(h + 1) * DH] = query_grad[h * SPAN:(h + 1) * SPAN]
        key_sum = lax.dot_general(grad_scores, query_all, contract_first,
                                  preferred_element_type=jnp.float32) * score_scale
        value_sum = lax.dot_general(weights_low, grad_all, contract_first,
                                    preferred_element_type=jnp.float32)

        slot_base = tiles * window_spans + base
        for w in range(window_spans):
            slot = index_ref[slot_base + w]
            part = slice(w * SPAN, (w + 1) * SPAN)
            buf_ref[slot, :, :DH] += key_sum[part]
            buf_ref[slot, :, DH:] += value_sum[part]

    my_half = index_ref[info]
    my_q = index_ref[info + 1]
    for shift, ref in enumerate((own_ref,) + tuple(send_refs)):
        target = my_half * half + (my_q ^ shift)
        other = (target + half) % (2 * half)
        for k, device in enumerate((target, other)):
            block = buf_ref[pl.ds(device * tiles, tiles)]
            ref[k, 0] = block.astype(ref.dtype)


def local(queries, key_rows, value_rows, out_grad, doc_start, span_order):
    local_rows = queries.shape[0]
    tiles = local_rows // SPAN
    head_count = queries.shape[1] // DH
    kv_count = key_rows.shape[1] // DH
    group_size = head_count // kv_count
    group_cols = group_size * DH
    score_scale = 1.0 / math.sqrt(DH)
    ctx_count = lax.axis_size("ctx")
    my_index = lax.axis_index("ctx")
    total_rows = local_rows * ctx_count
    slot_count = total_rows // SPAN
    reach = total_rows // 4 // SPAN
    window_spans = reach + 1
    window = window_spans * SPAN
    chunks = CHUNKS if kv_count % CHUNKS == 0 else 1
    chunk_heads = kv_count // chunks
    chunk_cols = chunk_heads * DH

    my_spans = lax.dynamic_slice_in_dim(span_order, my_index * tiles, tiles)
    window_span = my_spans[:, None] - reach + jnp.arange(window_spans, dtype=jnp.int32)[None, :]
    window_slot = jnp.sum(
        jnp.where(span_order[None, None, :] == window_span[:, :, None],
                  jnp.arange(slot_count, dtype=jnp.int32)[None, None, :], 0), axis=2)
    half = ctx_count // 2
    my_half = my_index // half
    my_q = my_index % half
    window_owner = window_slot // tiles
    owner_s = my_q ^ (window_owner % half)
    owner_k = (window_owner // half != my_half).astype(jnp.int32)
    window_row = owner_k * tiles + window_slot % tiles
    index_table = jnp.concatenate([owner_s.reshape(-1), window_slot.reshape(-1), my_spans,
                                   jnp.stack([my_half, my_q]).astype(jnp.int32),
                                   window_row.reshape(-1)])
    query_start = doc_start.reshape(tiles, SPAN, 1)

    def cross_pairs():
        return [(i, i ^ half) for i in range(ctx_count)]

    def half_pairs(shift):
        return [(i, (i // half) * half + ((i % half) ^ shift)) for i in range(ctx_count)]

    attended = None
    query_grad = None
    key_grads = []
    value_grads = []
    for chunk in range(chunks):
        cols = slice(chunk * chunk_cols, (chunk + 1) * chunk_cols)
        pair = jnp.concatenate([key_rows[:, cols], value_rows[:, cols]], axis=1)
        both = jnp.stack([pair, lax.ppermute(pair, "ctx", cross_pairs())])
        pieces = [both]
        for shift in range(1, half):
            pieces.append(lax.ppermute(both, "ctx", half_pairs(shift)))
        pieces = [piece.reshape(2 * tiles, SPAN, 2 * chunk_cols) for piece in pieces]

        aliased = chunk > 0
        head0 = chunk * chunk_heads
        in_specs = [
            pl.BlockSpec((tiles, SPAN, 1), lambda j, idx: (0, 0, 0)),
            pl.BlockSpec((local_rows, group_cols), lambda j, idx, h=head0: (0, h + j)),
            pl.BlockSpec((local_rows, group_cols), lambda j, idx, h=head0: (0, h + j)),
        ] + [pl.BlockSpec((2 * tiles, SPAN, DH), lambda j, idx: (0, 0, j))] * half + [
            pl.BlockSpec((2 * tiles, SPAN, DH), lambda j, idx, n=chunk_heads: (0, 0, n + j))
        ] * half
        operands = [index_table, query_start, queries, out_grad] + pieces + pieces
        aliases = {}
        if aliased:
            in_specs += [pl.BlockSpec(memory_space=pl.ANY), pl.BlockSpec(memory_space=pl.ANY)]
            operands += [attended, query_grad]
            aliases = {len(operands) - 2: 0, len(operands) - 1: 1}
        kernel = pl.pallas_call(
            lambda *refs, a=aliased: attention_kernel(
                *refs, group_size=group_size, window_spans=window_spans, tiles=tiles,
                half=half, score_scale=score_scale, aliased=a),
            grid_spec=pltpu.PrefetchScalarGridSpec(
                num_scalar_prefetch=1,
                grid=(chunk_heads,),
                in_specs=in_specs,
                out_specs=[
                    pl.BlockSpec((local_rows, group_cols), lambda j, idx, h=head0: (0, h + j)),
                    pl.BlockSpec((local_rows, group_cols), lambda j, idx, h=head0: (0, h + j)),
                ] + [pl.BlockSpec((2, 1, tiles, SPAN, 2 * DH), lambda j, idx: (0, j, 0, 0, 0))] * half,
                scratch_shapes=[pltpu.VMEM((slot_count, SPAN, 2 * DH), jnp.float32)],
            ),
            out_shape=[
                jax.ShapeDtypeStruct((local_rows, head_count * DH), jnp.bfloat16),
                jax.ShapeDtypeStruct((local_rows, head_count * DH), jnp.bfloat16),
                jax.ShapeDtypeStruct((2, chunk_heads, tiles, SPAN, 2 * DH), jnp.float32),
            ] + [jax.ShapeDtypeStruct((2, chunk_heads, tiles, SPAN, 2 * DH), jnp.bfloat16)] * (half - 1),
            input_output_aliases=aliases,
        )
        attended, query_grad, own_pack, *send_packs = kernel(*operands)

        pack_shape = (2, chunk_heads, local_rows, 2 * DH)
        summed = own_pack.reshape(pack_shape)
        for shift in range(1, half):
            summed = summed + lax.ppermute(
                send_packs[shift - 1].reshape(pack_shape), "ctx",
                half_pairs(shift)).astype(jnp.float32)
        summed = summed[0] + lax.ppermute(
            summed[1].astype(jnp.bfloat16), "ctx", cross_pairs()).astype(jnp.float32)
        key_grads.append(summed[:, :, :DH])
        value_grads.append(summed[:, :, DH:])

    def heads_to_cols(parts):
        stacked = jnp.concatenate(parts, axis=0)
        return stacked.transpose(1, 0, 2).reshape(local_rows, kv_count * DH).astype(jnp.bfloat16)

    return (attended, query_grad, heads_to_cols(key_grads), heads_to_cols(value_grads))


def solution(mesh):
    in_specs = (
        P(("groups", "ctx"), "head"),
        P(("groups", "ctx"), "head"),
        P(("groups", "ctx"), "head"),
        P(("groups", "ctx"), "head"),
        P(("groups", "ctx")),
        P("groups"),
    )
    out_specs = (
        P(("groups", "ctx"), "head"),
        P(("groups", "ctx"), "head"),
        P(("groups", "ctx"), "head"),
        P(("groups", "ctx"), "head"),
    )
    return jax.shard_map(local, mesh=mesh, in_specs=in_specs, out_specs=out_specs, check_vma=False)
```
